512 devices in a mesh: ctx: 64 (over z, x_lo, core), tp: 8 (over y, x_hi).
Axes of the slice: x: 4 (x_hi: 2, x_lo: 2; x = x_hi * 2 + x_lo), y: 4, z: 16, core: 2. Of those that a mesh axis runs over, the one named last changes fastest.
Arguments:
- queries: bfloat16 [8192, 4096], P('ctx', 'tp'), may hold values from -5 to 5
- keys: bfloat16 [8192, 1024], P('ctx', 'tp'), may hold values from -5 to 5
- values: bfloat16 [8192, 1024], P('ctx', 'tp'), may hold values from -6 to 6
- docs: int32 [8192], P('ctx'), may hold values from 0 to 11, never falling along the last dimension, each value on 1 to 4224 neighbouring positions
- out_weight: bfloat16 [4096, 4096], P('tp'), may hold values from -0.09375 to 0.09375
Outputs:
- mixed: bfloat16 [8192, 4096], P('ctx', 'tp')
The draws below stay inside these ranges and needn't reach their ends.
All inputs are finite; a program needn't handle non-finite values.
Results may differ from the reference program's by a relative error of at most 0.014.
Values may be sent and summed in bfloat16 or wider, within the bound.
No kernel may reach another device: no remote copies, remote signals or barrier semaphores. Data moves between devices by JAX's collectives and lax.ppermute only.
A program may use at most 64 MiB of HBM per device.

```python
import math
import jax
import jax.numpy as jnp
import numpy as np
from jax import lax

D = 4096
HEADS = 32
KV_HEADS = 8
HEAD_DIM = 128
TOK_DEV = 128
DOCS = 12
TOKENS = 8192


def draw_keys(key, part):
    shape = (TOKENS, KV_HEADS * HEAD_DIM)
    base = jnp.clip(1.7 * jax.random.normal(jax.random.fold_in(key, 11), shape, jnp.float32), -5.0, 5.0)
    return base.astype(jnp.bfloat16)


def draw_queries(key, part):
    shape = (TOKENS, HEADS * HEAD_DIM)
    base = jnp.clip(1.7 * jax.random.normal(jax.random.fold_in(key, 13), shape, jnp.float32), -5.0, 5.0)
    return base.astype(jnp.bfloat16)


def block_levels(stream_key, dims, pieces, low, top_value):
    def one(position, shards_of):
        draws = jax.random.uniform(jax.random.fold_in(jax.random.fold_in(stream_key, 6), position), (shards_of,), jnp.float32, low / len(pieces), top_value / len(pieces))
        return jnp.repeat(jnp.exp(draws), dims[position] // shards_of).reshape((-1,) + (1,) * (len(dims) - position - 1))

    factor_of = one(*pieces[0])
    for cut in pieces[1:]:
        factor_of = factor_of * one(*cut)
    return factor_of


def length_profile(count, total, bound, skew):
    loads = [(1 << 20) // math.isqrt(rank ** skew) + 1 for rank in range(2, count + 1)]
    surplus, given = total - bound - (count - 1), [1] * (count - 1)
    while surplus > 0:
        movable = [i for i in range(count - 1) if given[i] < bound]
        pool, left = sum([loads[i] for i in movable]), surplus
        for i in movable:
            addition = min(bound - given[i], max(1, left * loads[i] // pool), surplus)
            given[i] = given[i] + addition
            surplus = surplus - addition
    return np.array([bound] + given)


def ragged(key, number_of, total, limit, slope):
    if number_of == 2:
        one = jax.random.randint(key, (), max(1, total - limit), min(limit, total - 1) + 1)
        return jnp.stack([one, total - one])
    lengths = jnp.asarray(length_profile(number_of, total, limit, slope), jnp.int32)
    pairs = (number_of - 1) // 2
    giver, receiver = lengths[1:1 + 2 * pairs:2], lengths[2:2 + 2 * pairs:2]
    room = jnp.minimum(giver - 1, limit - receiver)
    moved = jax.random.randint(jax.random.fold_in(key, 1), (pairs,), 0, 1 << 20) % (room + 1)
    lengths = lengths.at[1:1 + 2 * pairs:2].set(giver - moved).at[2:2 + 2 * pairs:2].set(receiver + moved)
    return lengths[jax.random.permutation(jax.random.fold_in(key, 2), number_of)]


def scatter_about(stream_key, shape, scale, most, split=(), kind=jnp.bfloat16):
    values = scale * jax.random.normal(stream_key, shape, jnp.float32)
    if split:
        values = values * block_levels(stream_key, shape, split, -0.22, 0.18)
    return jnp.clip(values, -most, most).astype(kind)


def setup_inputs(seed: int = 0) -> dict:
    key_list = jax.random.split(jax.random.key(seed), 6)
    return {
        "queries": draw_queries(jax.random.fold_in(key_list[5], 71), 0),
        "keys": draw_keys(jax.random.fold_in(key_list[5], 71), 0),
        "values": scatter_about(key_list[2], (TOKENS, KV_HEADS * HEAD_DIM), 1.0, 6.0, ((0, 64), (1, 8))),
        "docs": jnp.searchsorted(jnp.cumsum(ragged(key_list[3], DOCS, TOKENS, TOKENS // 2 + TOK_DEV, 2)), jnp.arange(TOKENS), side="right").astype(jnp.int32),
        "out_weight": scatter_about(key_list[4], (HEADS * HEAD_DIM, D), (HEADS * HEAD_DIM) ** -0.5, 0.09375, ((0, 8),)),
    }


def reference(queries, keys, values, docs, out_weight):
    group_size = HEADS // KV_HEADS
    scale = 1.0 / math.sqrt(HEAD_DIM)
    key_float = keys.astype(jnp.float32).reshape(TOKENS, KV_HEADS, HEAD_DIM)
    value_float = values.astype(jnp.float32).reshape(TOKENS, KV_HEADS, HEAD_DIM)
    columns = jnp.arange(TOKENS, dtype=jnp.int32)

    def block(index):
        start = index * TOK_DEV
        query_block = lax.dynamic_slice_in_dim(queries, start, TOK_DEV, 0)
        query_block = query_block.astype(jnp.float32).reshape(TOK_DEV, KV_HEADS, group_size, HEAD_DIM)
        doc_block = lax.dynamic_slice_in_dim(docs, start, TOK_DEV, 0)
        row_positions = start + jnp.arange(TOK_DEV, dtype=jnp.int32)
        scores = jnp.einsum('igkd,jgd->gkij', query_block, key_float) * scale
        allowed = (columns[None, :] <= row_positions[:, None]) & (docs[None, :] == doc_block[:, None])
        peak = lax.optimization_barrier(jnp.max(jnp.where(allowed, scores, -1e+30), axis=-1, keepdims=True))
        weight = jnp.where(allowed, jnp.exp(scores - peak), 0.0)
        total = lax.optimization_barrier(jnp.sum(weight, axis=-1))
        rounded = lax.optimization_barrier(weight.astype(jnp.bfloat16)).astype(jnp.float32)
        summed = jnp.einsum('gkij,jgd->gkid', rounded, value_float) / total[..., None]
        summed = jnp.transpose(summed, (2, 0, 1, 3)).reshape(TOK_DEV, HEADS * HEAD_DIM)
        return summed.astype(jnp.bfloat16)
    attention = lax.map(block, jnp.arange(TOKENS // TOK_DEV, dtype=jnp.int32))
    attention = attention.reshape(TOKENS, HEADS * HEAD_DIM)
    return jnp.dot(attention, out_weight, preferred_element_type=jnp.float32).astype(jnp.bfloat16)
```

```python
import math

import jax
import jax.numpy as jnp
from jax import lax
from jax.sharding import PartitionSpec as P

HEAD_DIM = 128
MAX_DOC = 4224
PLANE = 4
neg_large = -1e30


def shards(queries, keys, values, docs, out_weight):
    rows = queries.shape[0]
    head_dim = HEAD_DIM
    group_size = queries.shape[1] // keys.shape[1]
    ctx = lax.psum(1, "ctx")
    tp = lax.psum(1, "tp")
    my_index = lax.axis_index("ctx")
    my_tp = lax.axis_index("tp")
    plane = my_index // PLANE
    slot = my_index % PLANE

    shards_back = -(-(MAX_DOC - 1) // rows)
    hops = min(-(-(shards_back + PLANE - 1) // PLANE), ctx // PLANE - 1)

    kv = jnp.concatenate([keys, values], axis=1)
    plane_kv = [kv]
    plane_docs = [docs]
    for offset in range(1, PLANE):
        perm = [(s, s ^ offset) for s in range(ctx)]
        plane_kv.append(lax.ppermute(kv, "ctx", perm))
        plane_docs.append(lax.ppermute(docs, "ctx", perm))
    block_kv = jnp.stack(plane_kv)
    block_docs = jnp.stack(plane_docs)

    forward = [(s, s + PLANE) for s in range(ctx - PLANE)]
    all_kv = [block_kv]
    all_docs = [block_docs]
    for hop in range(hops):
        block_kv = lax.ppermute(block_kv, "ctx", forward)
        block_docs = lax.ppermute(block_docs, "ctx", forward)
        all_kv.append(block_kv)
        all_docs.append(block_docs)
    all_kv = jnp.stack(all_kv)
    all_docs = jnp.stack(all_docs)
    count = all_kv.shape[0] * PLANE * rows

    hop_ids = jnp.arange(hops + 1, dtype=jnp.int32)[:, None, None]
    offsets = jnp.arange(PLANE, dtype=jnp.int32)[None, :, None]
    tokens = jnp.arange(rows, dtype=jnp.int32)[None, None, :]
    key_shard = PLANE * (plane - hop_ids) + (slot ^ offsets)
    key_pos = (key_shard * rows + tokens).reshape(count)
    key_doc = all_docs.reshape(count)
    key_part = all_kv[..., :head_dim].reshape(count, head_dim)
    value_part = all_kv[..., head_dim:].reshape(count, head_dim)

    query_pos = my_index * rows + jnp.arange(rows, dtype=jnp.int32)
    query = queries.reshape(rows, group_size, head_dim)
    scores = jnp.einsum("ihd,jd->hij", query, key_part, preferred_element_type=jnp.float32)
    scores = scores * (1.0 / math.sqrt(head_dim))
    allowed = (
        (key_pos[None, :] <= query_pos[:, None])
        & (key_pos[None, :] >= 0)
        & (key_doc[None, :] == docs[:, None])
    )
    peak = jnp.max(jnp.where(allowed, scores, neg_large), axis=-1)
    weight = jnp.where(allowed, jnp.exp(scores - peak[..., None]), 0.0)
    total = jnp.sum(weight, axis=-1)
    summed = jnp.einsum(
        "hij,jd->hid", weight.astype(jnp.bfloat16), value_part, preferred_element_type=jnp.float32
    )
    summed = summed / total[..., None]
    attention = jnp.transpose(summed, (1, 0, 2)).reshape(rows, group_size * head_dim)
    attention = attention.astype(jnp.bfloat16)

    partial_terms = jnp.dot(attention, out_weight, preferred_element_type=jnp.float32)
    width = partial_terms.shape[1] // tp
    chunks = jnp.transpose(partial_terms.reshape(rows, tp, width), (1, 0, 2))
    mixed = lax.dynamic_index_in_dim(chunks, my_tp, 0, keepdims=False)
    sent = chunks.astype(jnp.bfloat16)
    for shift in range(1, tp):
        piece = lax.dynamic_index_in_dim(sent, (my_tp + shift) % tp, 0, keepdims=False)
        perm = [(t, (t + shift) % tp) for t in range(tp)]
        mixed = mixed + lax.ppermute(piece, "tp", perm).astype(jnp.float32)
    return mixed.astype(jnp.bfloat16)


def solution(mesh):
    placed = (P("ctx", "tp"), P("ctx", "tp"), P("ctx", "tp"), P("ctx"), P("tp", None))
    return jax.shard_map(
        shards, mesh=mesh, in_specs=placed, out_specs=P("ctx", "tp"), check_vma=False
    )
```

```python
import math

import jax
import jax.numpy as jnp
from jax import lax
from jax.experimental import pallas as pl
from jax.experimental.pallas import tpu as pltpu
from jax.sharding import PartitionSpec as P

HEAD_DIM = 128
MAX_DOC = 4224
PLANE = 4
DOC_ROWS = 8
neg_large = -1e30


def attend_kernel(query_ref, block_ref, key_pos_ref, key_doc_ref, query_pos_ref,
                  query_doc_ref, weight_ref, out_ref):
    rows, width = query_ref.shape
    count, _, packed = block_ref.shape
    head_dim = packed // 2
    heads = width // head_dim
    tokens = count * rows
    key_part = block_ref[:, :rows, :head_dim].reshape(tokens, head_dim)
    value_part = block_ref[:, :rows, head_dim:].reshape(tokens, head_dim)
    key_pos = key_pos_ref[...]
    query_pos = query_pos_ref[...]
    allowed = (
        (key_pos <= query_pos) & (key_pos >= 0) & (key_doc_ref[...] == query_doc_ref[...])
    )
    scale = 1.0 / math.sqrt(head_dim)
    outputs = []
    for head in range(heads):
        query = query_ref[:, head * head_dim:(head + 1) * head_dim]
        scores = lax.dot_general(
            query, key_part, (((1,), (1,)), ((), ())), preferred_element_type=jnp.float32
        )
        scores = scores * scale
        peak = jnp.max(jnp.where(allowed, scores, neg_large), axis=1, keepdims=True)
        weight = jnp.where(allowed, jnp.exp(scores - peak), 0.0)
        total = jnp.sum(weight, axis=1, keepdims=True)
        summed = jnp.dot(
            weight.astype(jnp.bfloat16), value_part, preferred_element_type=jnp.float32
        )
        outputs.append((summed / total).astype(jnp.bfloat16))
    attention = jnp.concatenate(outputs, axis=1)
    partial_terms = jnp.dot(attention, weight_ref[...], preferred_element_type=jnp.float32)
    pieces, _, piece_width = out_ref.shape
    for piece in range(pieces):
        out_ref[piece] = partial_terms[:, piece * piece_width:(piece + 1) * piece_width].astype(
            out_ref.dtype
        )


def attend(query, blocks, key_pos, key_doc, query_pos, query_doc, out_weight, pieces):
    rows = query.shape[0]
    width = out_weight.shape[1]
    tokens = blocks.shape[0] * rows
    flops = 4 * rows * tokens * query.shape[1] + 2 * rows * query.shape[1] * width
    moved = blocks.size * 2 + out_weight.size * 2 + rows * width * 2
    vmem = pl.BlockSpec(memory_space=pltpu.VMEM)
    return pl.pallas_call(
        attend_kernel,
        out_shape=jax.ShapeDtypeStruct((pieces, rows, width // pieces), jnp.bfloat16),
        in_specs=[vmem] * 7,
        out_specs=vmem,
        cost_estimate=pl.CostEstimate(
            flops=flops, transcendentals=rows * tokens * query.shape[1] // HEAD_DIM,
            bytes_accessed=moved,
        ),
    )(query, blocks, key_pos, key_doc, query_pos, query_doc, out_weight)


def shards(queries, keys, values, docs, out_weight):
    rows = queries.shape[0]
    head_dim = HEAD_DIM
    ctx = lax.psum(1, "ctx")
    tp = lax.psum(1, "tp")
    my_index = lax.axis_index("ctx")
    my_tp = lax.axis_index("tp")
    plane = my_index // PLANE
    slot = my_index % PLANE

    shards_back = -(-(MAX_DOC - 1) // rows)
    hops = min(-(-(shards_back + PLANE - 1) // PLANE), ctx // PLANE - 1)

    doc_rows = jnp.zeros((DOC_ROWS, 2 * head_dim), jnp.bfloat16)
    doc_rows = doc_rows.at[0, :rows].set(docs.astype(jnp.bfloat16))
    block = jnp.concatenate([jnp.concatenate([keys, values], axis=1), doc_rows], axis=0)

    partner = lax.ppermute(block, "ctx", [(s, s ^ 2) for s in range(ctx)])
    pair = jnp.stack([block, partner])
    forward = [(s, s + PLANE) for s in range(ctx - PLANE)]
    collected = [pair]
    for hop in range(hops):
        pair = lax.ppermute(pair, "ctx", forward)
        collected.append(pair)
    mine = jnp.stack(collected)
    sibling = lax.ppermute(mine, "ctx", [(s, s ^ 1) for s in range(ctx)])
    blocks = jnp.stack([mine, sibling])
    count = blocks.shape[0] * blocks.shape[1] * blocks.shape[2]

    sib_ids = jnp.arange(2, dtype=jnp.int32)[:, None, None, None]
    hop_ids = jnp.arange(hops + 1, dtype=jnp.int32)[None, :, None, None]
    pair_ids = jnp.arange(2, dtype=jnp.int32)[None, None, :, None]
    tokens = jnp.arange(rows, dtype=jnp.int32)[None, None, None, :]
    key_shard = PLANE * (plane - hop_ids) + (slot ^ sib_ids ^ (2 * pair_ids))
    key_pos = (key_shard * rows + tokens).reshape(1, count * rows)
    blocks = blocks.reshape(count, rows + DOC_ROWS, 2 * head_dim)
    key_doc = blocks[:, rows, :rows].astype(jnp.int32).reshape(1, count * rows)

    query_pos = (my_index * rows + jnp.arange(rows, dtype=jnp.int32)).reshape(rows, 1)
    query_doc = docs.reshape(rows, 1)
    chunks = attend(queries, blocks, key_pos, key_doc, query_pos, query_doc, out_weight, tp)

    width = chunks.shape[-1]
    lanes = 2
    ring = tp // lanes
    my_lane = my_tp % lanes
    my_ring = my_tp // lanes
    chunks = chunks.reshape(ring, lanes, rows, width)
    keep = lax.dynamic_index_in_dim(chunks, my_lane, 1, keepdims=False)
    give = lax.dynamic_index_in_dim(chunks, 1 - my_lane, 1, keepdims=False)
    got = lax.ppermute(give, "tp", [(t, t ^ 1) for t in range(tp)])
    stage = keep.astype(jnp.float32) + got.astype(jnp.float32)
    mixed = lax.dynamic_index_in_dim(stage, my_ring, 0, keepdims=False)
    sent = stage.astype(jnp.bfloat16)
    for shift in range(1, ring):
        piece = lax.dynamic_index_in_dim(sent, (my_ring + shift) % ring, 0, keepdims=False)
        perm = [(t, (t + lanes * shift) % tp) for t in range(tp)]
        mixed = mixed + lax.ppermute(piece, "tp", perm).astype(jnp.float32)
    return mixed.astype(jnp.bfloat16)


def solution(mesh):
    placed = (P("ctx", "tp"), P("ctx", "tp"), P("ctx", "tp"), P("ctx"), P("tp", None))
    return jax.shard_map(
        shards, mesh=mesh, in_specs=placed, out_specs=P("ctx", "tp"), check_vma=False
    )
```

```python
import math

import jax
import jax.numpy as jnp
from jax import lax
from jax.experimental import pallas as pl
from jax.experimental.pallas import tpu as pltpu
from jax.sharding import PartitionSpec as P

HEAD_DIM = 128
MAX_DOC = 4224
PLANE = 4
DOC_ROWS = 8
neg_large = -1e30


def attend_kernel(*refs):
    query_ref = refs[0]
    block_refs = refs[1:-6]
    key_pos_ref, key_doc_ref, query_pos_ref, query_doc_ref, weight_ref, out_ref = refs[-6:]
    rows, width = query_ref.shape
    head_dim = block_refs[0].shape[-1] // 2
    heads = width // head_dim
    key_part = jnp.concatenate(
        [ref[:, :rows, :head_dim].reshape(ref.shape[0] * rows, head_dim) for ref in block_refs],
        axis=0,
    )
    value_part = jnp.concatenate(
        [ref[:, :rows, head_dim:].reshape(ref.shape[0] * rows, head_dim) for ref in block_refs],
        axis=0,
    )
    key_pos = key_pos_ref[...]
    query_pos = query_pos_ref[...]
    allowed = (
        (key_pos <= query_pos) & (key_pos >= 0) & (key_doc_ref[...] == query_doc_ref[...])
    )
    bias = jnp.where(allowed, 0.0, neg_large)
    scale = 1.0 / math.sqrt(head_dim)
    outputs = []
    for head in range(heads):
        query = query_ref[:, head * head_dim:(head + 1) * head_dim]
        scores = lax.dot_general(
            query, key_part, (((1,), (1,)), ((), ())), preferred_element_type=jnp.float32
        )
        scores = scores * scale + bias
        peak = jnp.max(scores, axis=1, keepdims=True)
        weight = jnp.exp(scores - peak)
        total = jnp.sum(weight, axis=1, keepdims=True)
        summed = jnp.dot(
            weight.astype(jnp.bfloat16), value_part, preferred_element_type=jnp.float32
        )
        outputs.append((summed / total).astype(jnp.bfloat16))
    attention = jnp.concatenate(outputs, axis=1)
    partial_terms = jnp.dot(attention, weight_ref[...], preferred_element_type=jnp.float32)
    pieces, _, piece_width = out_ref.shape
    for piece in range(pieces):
        out_ref[piece] = partial_terms[:, piece * piece_width:(piece + 1) * piece_width].astype(
            out_ref.dtype
        )


def attend(query, blocks, key_pos, key_doc, query_pos, query_doc, out_weight, pieces):
    rows = query.shape[0]
    width = out_weight.shape[1]
    tokens = key_pos.shape[1]
    flops = 4 * rows * tokens * query.shape[1] + 2 * rows * query.shape[1] * width
    moved = sum(b.size for b in blocks) * 2 + out_weight.size * 2 + rows * width * 2
    vmem = pl.BlockSpec(memory_space=pltpu.VMEM)
    return pl.pallas_call(
        attend_kernel,
        out_shape=jax.ShapeDtypeStruct((pieces, rows, width // pieces), jnp.bfloat16),
        in_specs=[vmem] * (6 + len(blocks)),
        out_specs=vmem,
        cost_estimate=pl.CostEstimate(
            flops=flops, transcendentals=rows * tokens * query.shape[1] // HEAD_DIM,
            bytes_accessed=moved,
        ),
    )(query, *blocks, key_pos, key_doc, query_pos, query_doc, out_weight)


def shards(queries, keys, values, docs, out_weight):
    rows = queries.shape[0]
    head_dim = HEAD_DIM
    ctx = lax.psum(1, "ctx")
    tp = lax.psum(1, "tp")
    my_index = lax.axis_index("ctx")
    my_tp = lax.axis_index("tp")
    plane = my_index // PLANE
    slot = my_index % PLANE

    shards_back = -(-(MAX_DOC - 1) // rows)
    hops = min(-(-(shards_back + PLANE - 1) // PLANE), ctx // PLANE - 1)

    doc_rows = jnp.zeros((DOC_ROWS, 2 * head_dim), jnp.bfloat16)
    doc_rows = doc_rows.at[0, :rows].set(docs.astype(jnp.bfloat16))
    block = jnp.concatenate([jnp.concatenate([keys, values], axis=1), doc_rows], axis=0)

    partner = lax.ppermute(block, "ctx", [(s, s ^ 2) for s in range(ctx)])
    pair = jnp.stack([block, partner])
    forward = [(s, s + PLANE) for s in range(ctx - PLANE)]
    collected = [pair]
    for hop in range(hops):
        pair = lax.ppermute(pair, "ctx", forward)
        collected.append(pair)
    early = (hops + 2) // 2
    swap = [(s, s ^ 1) for s in range(ctx)]
    blocks, key_pos, key_doc = [], [], []
    tokens = jnp.arange(rows, dtype=jnp.int32)[None, None, :]
    pair_ids = jnp.arange(2, dtype=jnp.int32)[None, :, None]
    for first, last in ((0, early), (early, hops + 1)):
        mine = jnp.stack(collected[first:last])
        sibling = lax.ppermute(mine, "ctx", swap)
        hop_ids = jnp.arange(first, last, dtype=jnp.int32)[:, None, None]
        for piece, flip in ((mine, 0), (sibling, 1)):
            key_shard = PLANE * (plane - hop_ids) + (slot ^ flip ^ (2 * pair_ids))
            key_pos.append((key_shard * rows + tokens).reshape(1, -1))
            piece = piece.reshape(-1, rows + DOC_ROWS, 2 * head_dim)
            key_doc.append(piece[:, rows, :rows].astype(jnp.int32).reshape(1, -1))
            blocks.append(piece)
    key_pos = jnp.concatenate(key_pos, axis=1)
    key_doc = jnp.concatenate(key_doc, axis=1)

    query_pos = (my_index * rows + jnp.arange(rows, dtype=jnp.int32)).reshape(rows, 1)
    query_doc = docs.reshape(rows, 1)
    chunks = attend(queries, blocks, key_pos, key_doc, query_pos, query_doc, out_weight, tp)

    received = lax.all_to_all(chunks, "tp", 0, 0, tiled=True)
    mixed = jnp.sum(received.astype(jnp.float32), axis=0)
    return mixed.astype(jnp.bfloat16)


def solution(mesh):
    placed = (P("ctx", "tp"), P("ctx", "tp"), P("ctx", "tp"), P("ctx"), P("tp", None))
    return jax.shard_map(
        shards, mesh=mesh, in_specs=placed, out_specs=P("ctx", "tp"), check_vma=False
    )
```

```python
import math

import jax
import jax.numpy as jnp
from jax import lax
from jax.experimental import pallas as pl
from jax.experimental.pallas import tpu as pltpu
from jax.sharding import PartitionSpec as P

HEAD_DIM = 128
MAX_DOC = 4224
PLANE = 4
DOC_ROWS = 8
neg_large = -1e30


def partial_kernel(query_ref, block_ref, key_pos_ref, key_doc_ref, query_pos_ref,
                   query_doc_ref, out_ref, stats_ref):
    rows = query_pos_ref.shape[0]
    width = query_ref.shape[1]
    count, _, packed = block_ref.shape
    head_dim = packed // 2
    heads = width // head_dim
    tokens = count * rows
    key_part = block_ref[:, :rows, :head_dim].reshape(tokens, head_dim)
    value_part = block_ref[:, :rows, head_dim:].reshape(tokens, head_dim)
    allowed = (
        (key_pos_ref[...] <= query_pos_ref[...])
        & (key_pos_ref[...] >= 0)
        & (key_doc_ref[...] == query_doc_ref[...])
    )
    scale = 1.0 / math.sqrt(head_dim)
    for head in range(heads):
        query = query_ref[:rows, head * head_dim:(head + 1) * head_dim]
        scores = lax.dot_general(
            query, key_part, (((1,), (1,)), ((), ())), preferred_element_type=jnp.float32
        )
        scores = scores * scale
        peak = jnp.max(jnp.where(allowed, scores, neg_large), axis=1, keepdims=True)
        weight = jnp.where(allowed, jnp.exp(scores - peak), 0.0)
        total = jnp.sum(weight, axis=1, keepdims=True)
        summed = jnp.dot(
            weight.astype(jnp.bfloat16), value_part, preferred_element_type=jnp.float32
        )
        normed = jnp.where(total > 0.0, summed / jnp.maximum(total, 1e-30), 0.0)
        out_ref[:, head * head_dim:(head + 1) * head_dim] = normed.astype(out_ref.dtype)
        stats_ref[:, head:head + 1] = peak
        stats_ref[:, heads + head:heads + head + 1] = total


def partial(query, blocks, key_pos, key_doc, query_pos, query_doc, out_dtype):
    rows = query_pos.shape[0]
    width = query.shape[1]
    heads = width // HEAD_DIM
    tokens = key_pos.shape[1]
    vmem = pl.BlockSpec(memory_space=pltpu.VMEM)
    return pl.pallas_call(
        partial_kernel,
        out_shape=(
            jax.ShapeDtypeStruct((rows, width), out_dtype),
            jax.ShapeDtypeStruct((rows, 2 * heads), jnp.float32),
        ),
        in_specs=[vmem] * 6,
        out_specs=(vmem, vmem),
        cost_estimate=pl.CostEstimate(
            flops=4 * rows * tokens * width, transcendentals=rows * tokens * heads,
            bytes_accessed=blocks.size * 2 + query.size * 2 + rows * width * 4,
        ),
    )(query, blocks, key_pos, key_doc, query_pos, query_doc)


def merge_kernel(near_ref, near_stats_ref, far_ref, far_stats_ref, weight_ref, out_ref):
    rows, width = near_ref.shape
    heads = near_stats_ref.shape[1] // 2
    head_dim = width // heads
    outputs = []
    for head in range(heads):
        near_peak = near_stats_ref[:, head:head + 1]
        near_total = near_stats_ref[:, heads + head:heads + head + 1]
        far_peak = far_stats_ref[:, head:head + 1]
        far_total = far_stats_ref[:, heads + head:heads + head + 1]
        peak = jnp.maximum(near_peak, far_peak)
        near_share = near_total * jnp.exp(near_peak - peak)
        far_share = far_total * jnp.exp(far_peak - peak)
        columns = slice(head * head_dim, (head + 1) * head_dim)
        summed = (
            near_ref[:, columns].astype(jnp.float32) * near_share
            + far_ref[:, columns].astype(jnp.float32) * far_share
        )
        outputs.append((summed / (near_share + far_share)).astype(jnp.bfloat16))
    attention = jnp.concatenate(outputs, axis=1)
    partial_terms = jnp.dot(attention, weight_ref[...], preferred_element_type=jnp.float32)
    pieces, _, piece_width = out_ref.shape
    for piece in range(pieces):
        out_ref[piece] = partial_terms[:, piece * piece_width:(piece + 1) * piece_width].astype(
            out_ref.dtype
        )


def merge(near, near_stats, far, far_stats, out_weight, pieces):
    rows = near.shape[0]
    width = out_weight.shape[1]
    vmem = pl.BlockSpec(memory_space=pltpu.VMEM)
    return pl.pallas_call(
        merge_kernel,
        out_shape=jax.ShapeDtypeStruct((pieces, rows, width // pieces), jnp.bfloat16),
        in_specs=[vmem] * 5,
        out_specs=vmem,
        cost_estimate=pl.CostEstimate(
            flops=2 * rows * near.shape[1] * width, transcendentals=0,
            bytes_accessed=out_weight.size * 2 + rows * width * 2,
        ),
    )(near, near_stats, far, far_stats, out_weight)


def shards(queries, keys, values, docs, out_weight):
    rows = queries.shape[0]
    head_dim = HEAD_DIM
    ctx = lax.psum(1, "ctx")
    tp = lax.psum(1, "tp")
    my_index = lax.axis_index("ctx")
    plane = my_index // PLANE
    slot = my_index % PLANE
    planes = ctx // PLANE

    shards_back = -(-(MAX_DOC - 1) // rows)
    reach = min(-(-(shards_back + PLANE - 1) // PLANE), planes - 1)
    hops = reach // 2
    far = hops + 1

    doc_rows = jnp.zeros((DOC_ROWS, 2 * head_dim), jnp.bfloat16)
    doc_rows = doc_rows.at[0, :rows].set(docs.astype(jnp.bfloat16))
    block = jnp.concatenate([jnp.concatenate([keys, values], axis=1), doc_rows], axis=0)

    query_docs = jnp.zeros((DOC_ROWS, queries.shape[1]), jnp.bfloat16)
    query_docs = query_docs.at[0, :rows].set(docs.astype(jnp.bfloat16))
    packed_queries = jnp.concatenate([queries, query_docs], axis=0)
    back = [(s, s - PLANE * far) for s in range(PLANE * far, ctx)]
    visiting = lax.ppermute(packed_queries, "ctx", back)

    plane_blocks = [block]
    for offset in range(1, PLANE):
        plane_blocks.append(lax.ppermute(block, "ctx", [(s, s ^ offset) for s in range(ctx)]))
    current = jnp.stack(plane_blocks)
    forward = [(s, s + PLANE) for s in range(ctx - PLANE)]
    collected = [current]
    for hop in range(hops):
        current = lax.ppermute(current, "ctx", forward)
        collected.append(current)
    blocks = jnp.stack(collected)

    hop_ids = jnp.arange(hops + 1, dtype=jnp.int32)[:, None, None]
    offsets = jnp.arange(PLANE, dtype=jnp.int32)[None, :, None]
    tokens = jnp.arange(rows, dtype=jnp.int32)[None, None, :]
    key_shard = PLANE * (plane - hop_ids) + (slot ^ offsets)
    key_pos = (key_shard * rows + tokens).reshape(1, -1)
    blocks = blocks.reshape(-1, rows + DOC_ROWS, 2 * head_dim)
    key_doc = blocks[:, rows, :rows].astype(jnp.int32).reshape(1, -1)

    offsets_in_shard = jnp.arange(rows, dtype=jnp.int32).reshape(rows, 1)
    visit_pos = (my_index + PLANE * far) * rows + offsets_in_shard
    visit_doc = visiting[rows, :rows].astype(jnp.int32).reshape(rows, 1)
    visit_out, visit_stats = partial(
        visiting, blocks, key_pos, key_doc, visit_pos, visit_doc, jnp.bfloat16
    )
    ahead = [(s, s + PLANE * far) for s in range(ctx - PLANE * far)]
    far_out = lax.ppermute(visit_out, "ctx", ahead)
    far_stats = lax.ppermute(visit_stats, "ctx", ahead)

    query_pos = my_index * rows + offsets_in_shard
    near_out, near_stats = partial(
        queries, blocks, key_pos, key_doc, query_pos, docs.reshape(rows, 1), jnp.float32
    )
    has_far = plane >= far
    heads = near_stats.shape[1] // 2
    lane = jnp.arange(2 * heads, dtype=jnp.int32)[None, :]
    far_stats = jnp.where(has_far, far_stats, jnp.where(lane < heads, neg_large, 0.0))
    chunks = merge(near_out, near_stats, far_out, far_stats, out_weight, tp)

    received = lax.all_to_all(chunks, "tp", 0, 0, tiled=True)
    mixed = jnp.sum(received.astype(jnp.float32), axis=0)
    return mixed.astype(jnp.bfloat16)


def solution(mesh):
    placed = (P("ctx", "tp"), P("ctx", "tp"), P("ctx", "tp"), P("ctx"), P("tp", None))
    return jax.shard_map(
        shards, mesh=mesh, in_specs=placed, out_specs=P("ctx", "tp"), check_vma=False
    )
```

```python
import math

import jax
import jax.numpy as jnp
from jax import lax
from jax.experimental import pallas as pl
from jax.experimental.pallas import tpu as pltpu
from jax.sharding import PartitionSpec as P

HEAD_DIM = 128
MAX_DOC = 4224
PLANE = 4
DOC_ROWS = 8
neg_large = -1e30


def step_kernel(*refs):
    (own_ref, visit_ref, block_ref, key_pos_ref, key_doc_ref, own_pos_ref, own_doc_ref,
     visit_pos_ref, visit_doc_ref) = refs[:9]
    states_in = refs[9:15]
    states_out = refs[15:]
    rows = own_pos_ref.shape[0]
    width = own_ref.shape[1]
    count, _, packed = block_ref.shape
    head_dim = packed // 2
    heads = width // head_dim
    tokens = count * rows
    key_part = block_ref[:, :rows, :head_dim].reshape(tokens, head_dim)
    value_part = block_ref[:, :rows, head_dim:].reshape(tokens, head_dim)
    key_pos = key_pos_ref[...]
    key_doc = key_doc_ref[...]
    scale = 1.0 / math.sqrt(head_dim)
    sets = (
        (own_ref, own_pos_ref, own_doc_ref, states_in[0:3], states_out[0:3]),
        (visit_ref, visit_pos_ref, visit_doc_ref, states_in[3:6], states_out[3:6]),
    )
    for query_ref, pos_ref, doc_ref, (peak_in, total_in, acc_in), (peak_out, total_out,
                                                                  acc_out) in sets:
        allowed = (key_pos <= pos_ref[...]) & (key_pos >= 0) & (key_doc == doc_ref[...])
        for head in range(heads):
            columns = slice(head * head_dim, (head + 1) * head_dim)
            query = query_ref[:rows, columns]
            scores = lax.dot_general(
                query, key_part, (((1,), (1,)), ((), ())), preferred_element_type=jnp.float32
            )
            scores = scores * scale
            old_peak = peak_in[:, head:head + 1]
            block_peak = jnp.max(jnp.where(allowed, scores, neg_large), axis=1, keepdims=True)
            peak = jnp.maximum(old_peak, block_peak)
            rescale = jnp.exp(old_peak - peak)
            weight = jnp.where(allowed, jnp.exp(scores - peak), 0.0)
            total = total_in[:, head:head + 1] * rescale + jnp.sum(weight, axis=1, keepdims=True)
            update = jnp.dot(
                weight.astype(jnp.bfloat16), value_part, preferred_element_type=jnp.float32
            )
            acc_out[:, columns] = acc_in[:, columns] * rescale + update
            peak_out[:, head:head + 1] = peak
            total_out[:, head:head + 1] = total


def step(own, visiting, block, key_pos, key_doc, own_pos, own_doc, visit_pos, visit_doc,
         states):
    rows = own_pos.shape[0]
    width = own.shape[1]
    heads = width // HEAD_DIM
    tokens = key_pos.shape[1]
    vmem = pl.BlockSpec(memory_space=pltpu.VMEM)
    shapes = tuple(jax.ShapeDtypeStruct(x.shape, x.dtype) for x in states)
    return pl.pallas_call(
        step_kernel,
        out_shape=shapes,
        in_specs=[vmem] * (9 + len(states)),
        out_specs=tuple([vmem] * len(states)),
        input_output_aliases={9 + i: i for i in range(len(states))},
        cost_estimate=pl.CostEstimate(
            flops=8 * rows * tokens * width, transcendentals=2 * rows * tokens * heads,
            bytes_accessed=block.size * 2 + 4 * rows * width * 4,
        ),
    )(own, visiting, block, key_pos, key_doc, own_pos, own_doc, visit_pos, visit_doc, *states)


def merge_kernel(near_peak_ref, near_total_ref, near_ref, far_ref, far_stats_ref, weight_ref,
                 out_ref):
    rows, width = near_ref.shape
    heads = near_peak_ref.shape[1]
    head_dim = width // heads
    outputs = []
    for head in range(heads):
        near_peak = near_peak_ref[:, head:head + 1]
        near_total = near_total_ref[:, head:head + 1]
        far_peak = far_stats_ref[:, head:head + 1]
        far_total = far_stats_ref[:, heads + head:heads + head + 1]
        peak = jnp.maximum(near_peak, far_peak)
        near_scale = jnp.exp(near_peak - peak)
        near_share = near_total * near_scale
        far_share = far_total * jnp.exp(far_peak - peak)
        columns = slice(head * head_dim, (head + 1) * head_dim)
        summed = (
            near_ref[:, columns] * near_scale
            + far_ref[:, columns].astype(jnp.float32) * far_share
        )
        outputs.append((summed / (near_share + far_share)).astype(jnp.bfloat16))
    attention = jnp.concatenate(outputs, axis=1)
    partial_terms = jnp.dot(attention, weight_ref[...], preferred_element_type=jnp.float32)
    pieces, _, piece_width = out_ref.shape
    for piece in range(pieces):
        out_ref[piece] = partial_terms[:, piece * piece_width:(piece + 1) * piece_width].astype(
            out_ref.dtype
        )


def merge(near_peak, near_total, near, far, far_stats, out_weight, pieces):
    rows = near.shape[0]
    width = out_weight.shape[1]
    vmem = pl.BlockSpec(memory_space=pltpu.VMEM)
    return pl.pallas_call(
        merge_kernel,
        out_shape=jax.ShapeDtypeStruct((pieces, rows, width // pieces), jnp.bfloat16),
        in_specs=[vmem] * 6,
        out_specs=vmem,
        cost_estimate=pl.CostEstimate(
            flops=2 * rows * near.shape[1] * width, transcendentals=0,
            bytes_accessed=out_weight.size * 2 + rows * width * 2,
        ),
    )(near_peak, near_total, near, far, far_stats, out_weight)


def shards(queries, keys, values, docs, out_weight):
    rows = queries.shape[0]
    head_dim = HEAD_DIM
    ctx = lax.psum(1, "ctx")
    tp = lax.psum(1, "tp")
    my_index = lax.axis_index("ctx")
    plane = my_index // PLANE
    slot = my_index % PLANE
    planes = ctx // PLANE

    shards_back = -(-(MAX_DOC - 1) // rows)
    reach = min(-(-(shards_back + PLANE - 1) // PLANE), planes - 1)
    hops = reach // 2
    far = hops + 1

    doc_rows = jnp.zeros((DOC_ROWS, 2 * head_dim), jnp.bfloat16)
    doc_rows = doc_rows.at[0, :rows].set(docs.astype(jnp.bfloat16))
    block = jnp.concatenate([jnp.concatenate([keys, values], axis=1), doc_rows], axis=0)

    query_docs = jnp.zeros((DOC_ROWS, queries.shape[1]), jnp.bfloat16)
    query_docs = query_docs.at[0, :rows].set(docs.astype(jnp.bfloat16))
    packed_queries = jnp.concatenate([queries, query_docs], axis=0)
    back = [(s, s - PLANE * far) for s in range(PLANE * far, ctx)]
    visiting = lax.ppermute(packed_queries, "ctx", back)

    plane_blocks = [block]
    for offset in range(1, PLANE):
        plane_blocks.append(lax.ppermute(block, "ctx", [(s, s ^ offset) for s in range(ctx)]))
    current = jnp.stack(plane_blocks)
    offsets_in_shard = jnp.arange(rows, dtype=jnp.int32).reshape(rows, 1)
    visit_pos = (my_index + PLANE * far) * rows + offsets_in_shard
    visit_doc = visiting[rows, :rows].astype(jnp.int32).reshape(rows, 1)
    own_pos = my_index * rows + offsets_in_shard
    own_doc = docs.reshape(rows, 1)
    heads = queries.shape[1] // head_dim
    empty = (
        jnp.full((rows, heads), neg_large, jnp.float32),
        jnp.zeros((rows, heads), jnp.float32),
        jnp.zeros((rows, queries.shape[1]), jnp.float32),
    )
    states = empty + empty

    offsets = jnp.arange(PLANE, dtype=jnp.int32)[:, None]
    tokens = jnp.arange(rows, dtype=jnp.int32)[None, :]
    forward = [(s, s + PLANE) for s in range(ctx - PLANE)]
    for hop in range(hops + 1):
        if hop:
            current = lax.ppermute(current, "ctx", forward)
        key_shard = PLANE * (plane - hop) + (slot ^ offsets)
        key_pos = (key_shard * rows + tokens).reshape(1, -1)
        key_doc = current[:, rows, :rows].astype(jnp.int32).reshape(1, -1)
        states = step(
            queries, visiting, current, key_pos, key_doc, own_pos, own_doc, visit_pos,
            visit_doc, states,
        )

    near_peak, near_total, near_acc, visit_peak, visit_total, visit_acc = states
    visit_out = jnp.where(
        visit_total[:, :, None] > 0.0,
        visit_acc.reshape(rows, heads, head_dim)
        / jnp.maximum(visit_total, 1e-30)[:, :, None],
        0.0,
    ).reshape(rows, heads * head_dim).astype(jnp.bfloat16)
    visit_stats = jnp.concatenate([visit_peak, visit_total], axis=1)
    ahead = [(s, s + PLANE * far) for s in range(ctx - PLANE * far)]
    far_out = lax.ppermute(visit_out, "ctx", ahead)
    far_stats = lax.ppermute(visit_stats, "ctx", ahead)

    has_far = plane >= far
    lane = jnp.arange(2 * heads, dtype=jnp.int32)[None, :]
    far_stats = jnp.where(has_far, far_stats, jnp.where(lane < heads, neg_large, 0.0))
    chunks = merge(near_peak, near_total, near_acc, far_out, far_stats, out_weight, tp)

    received = lax.all_to_all(chunks, "tp", 0, 0, tiled=True)
    mixed = jnp.sum(received.astype(jnp.float32), axis=0)
    return mixed.astype(jnp.bfloat16)


def solution(mesh):
    placed = (P("ctx", "tp"), P("ctx", "tp"), P("ctx", "tp"), P("ctx"), P("tp", None))
    return jax.shard_map(
        shards, mesh=mesh, in_specs=placed, out_specs=P("ctx", "tp"), check_vma=False
    )
```

```python
import math

import jax
import jax.numpy as jnp
from jax import lax
from jax.experimental import pallas as pl
from jax.experimental.pallas import tpu as pltpu
from jax.sharding import PartitionSpec as P

HEAD_DIM = 128
MAX_DOC = 4224
PLANE = 4
DOC_ROWS = 8
neg_large = -1e30


def partial_kernel(query_ref, block_ref, key_pos_ref, key_doc_ref, query_pos_ref,
                   query_doc_ref, out_ref, stats_ref):
    rows = query_pos_ref.shape[0]
    width = query_ref.shape[1]
    count, _, packed = block_ref.shape
    head_dim = packed // 2
    heads = width // head_dim
    tokens = count * rows
    key_part = block_ref[:, :rows, :head_dim].reshape(tokens, head_dim)
    value_part = block_ref[:, :rows, head_dim:].reshape(tokens, head_dim)
    allowed = (
        (key_pos_ref[...] <= query_pos_ref[...])
        & (key_pos_ref[...] >= 0)
        & (key_doc_ref[...] == query_doc_ref[...])
    )
    scale = 1.0 / math.sqrt(head_dim)
    for head in range(heads):
        query = query_ref[:rows, head * head_dim:(head + 1) * head_dim]
        scores = lax.dot_general(
            query, key_part, (((1,), (1,)), ((), ())), preferred_element_type=jnp.float32
        )
        scores = scores * scale
        peak = jnp.max(jnp.where(allowed, scores, neg_large), axis=1, keepdims=True)
        weight = jnp.where(allowed, jnp.exp(scores - peak), 0.0)
        total = jnp.sum(weight, axis=1, keepdims=True)
        summed = jnp.dot(
            weight.astype(jnp.bfloat16), value_part, preferred_element_type=jnp.float32
        )
        normed = jnp.where(total > 0.0, summed / jnp.maximum(total, 1e-30), 0.0)
        out_ref[:, head * head_dim:(head + 1) * head_dim] = normed.astype(out_ref.dtype)
        stats_ref[:, head:head + 1] = peak
        stats_ref[:, heads + head:heads + head + 1] = total


def partial(query, blocks, key_pos, key_doc, query_pos, query_doc, out_dtype):
    rows = query_pos.shape[0]
    width = query.shape[1]
    heads = width // HEAD_DIM
    tokens = key_pos.shape[1]
    vmem = pl.BlockSpec(memory_space=pltpu.VMEM)
    return pl.pallas_call(
        partial_kernel,
        out_shape=(
            jax.ShapeDtypeStruct((rows, width), out_dtype),
            jax.ShapeDtypeStruct((rows, 2 * heads), jnp.float32),
        ),
        in_specs=[vmem] * 6,
        out_specs=(vmem, vmem),
        cost_estimate=pl.CostEstimate(
            flops=4 * rows * tokens * width, transcendentals=rows * tokens * heads,
            bytes_accessed=blocks.size * 2 + query.size * 2 + rows * width * 4,
        ),
    )(query, blocks, key_pos, key_doc, query_pos, query_doc)


def merge_kernel(near_ref, near_stats_ref, far_ref, far_stats_ref, weight_ref, out_ref):
    rows, width = near_ref.shape
    heads = near_stats_ref.shape[1] // 2
    head_dim = width // heads
    outputs = []
    for head in range(heads):
        near_peak = near_stats_ref[:, head:head + 1]
        near_total = near_stats_ref[:, heads + head:heads + head + 1]
        far_peak = far_stats_ref[:, head:head + 1]
        far_total = far_stats_ref[:, heads + head:heads + head + 1]
        peak = jnp.maximum(near_peak, far_peak)
        near_share = near_total * jnp.exp(near_peak - peak)
        far_share = far_total * jnp.exp(far_peak - peak)
        columns = slice(head * head_dim, (head + 1) * head_dim)
        summed = (
            near_ref[:, columns].astype(jnp.float32) * near_share
            + far_ref[:, columns].astype(jnp.float32) * far_share
        )
        outputs.append((summed / (near_share + far_share)).astype(jnp.bfloat16))
    attention = jnp.concatenate(outputs, axis=1)
    partial_terms = jnp.dot(attention, weight_ref[...], preferred_element_type=jnp.float32)
    pieces, _, piece_width = out_ref.shape
    for piece in range(pieces):
        out_ref[piece] = partial_terms[:, piece * piece_width:(piece + 1) * piece_width].astype(
            out_ref.dtype
        )


def merge(near, near_stats, far, far_stats, out_weight, pieces):
    rows = near.shape[0]
    width = out_weight.shape[1]
    vmem = pl.BlockSpec(memory_space=pltpu.VMEM)
    return pl.pallas_call(
        merge_kernel,
        out_shape=jax.ShapeDtypeStruct((pieces, rows, width // pieces), jnp.bfloat16),
        in_specs=[vmem] * 5,
        out_specs=vmem,
        cost_estimate=pl.CostEstimate(
            flops=2 * rows * near.shape[1] * width, transcendentals=0,
            bytes_accessed=out_weight.size * 2 + rows * width * 2,
        ),
    )(near, near_stats, far, far_stats, out_weight)


def shards(queries, keys, values, docs, out_weight):
    rows = queries.shape[0]
    head_dim = HEAD_DIM
    ctx = lax.psum(1, "ctx")
    tp = lax.psum(1, "tp")
    my_index = lax.axis_index("ctx")
    plane = my_index // PLANE
    slot = my_index % PLANE
    planes = ctx // PLANE

    shards_back = -(-(MAX_DOC - 1) // rows)
    reach = min(-(-(shards_back + PLANE - 1) // PLANE), planes - 1)
    hops = reach // 2
    far = hops + 1

    doc_rows = jnp.zeros((DOC_ROWS, 2 * head_dim), jnp.bfloat16)
    doc_rows = doc_rows.at[0, :rows].set(docs.astype(jnp.bfloat16))
    block = jnp.concatenate([jnp.concatenate([keys, values], axis=1), doc_rows], axis=0)

    query_docs = jnp.zeros((DOC_ROWS, queries.shape[1]), jnp.bfloat16)
    query_docs = query_docs.at[0, :rows].set(docs.astype(jnp.bfloat16))
    packed_queries = jnp.concatenate([queries, query_docs], axis=0)
    back = [(s, s - PLANE * far) for s in range(PLANE * far, ctx)]
    visiting = lax.ppermute(packed_queries, "ctx", back)

    plane_blocks = [block]
    for offset in range(1, PLANE):
        plane_blocks.append(lax.ppermute(block, "ctx", [(s, s ^ offset) for s in range(ctx)]))
    current = jnp.stack(plane_blocks)
    forward = [(s, s + PLANE) for s in range(ctx - PLANE)]
    collected = [current]
    for hop in range(hops):
        current = lax.ppermute(current, "ctx", forward)
        collected.append(current)
    blocks = jnp.stack(collected)

    hop_ids = jnp.arange(hops + 1, dtype=jnp.int32)[:, None, None]
    offsets = jnp.arange(PLANE, dtype=jnp.int32)[None, :, None]
    tokens = jnp.arange(rows, dtype=jnp.int32)[None, None, :]
    key_shard = PLANE * (plane - hop_ids) + (slot ^ offsets)
    key_pos = (key_shard * rows + tokens).reshape(1, -1)
    blocks = blocks.reshape(-1, rows + DOC_ROWS, 2 * head_dim)
    key_doc = blocks[:, rows, :rows].astype(jnp.int32).reshape(1, -1)

    offsets_in_shard = jnp.arange(rows, dtype=jnp.int32).reshape(rows, 1)
    visit_pos = (my_index + PLANE * far) * rows + offsets_in_shard
    visit_doc = visiting[rows, :rows].astype(jnp.int32).reshape(rows, 1)
    visit_out, visit_stats = partial(
        visiting, blocks, key_pos, key_doc, visit_pos, visit_doc, jnp.bfloat16
    )
    stats_rows = visit_stats.T
    parts = []
    for part in range(3):
        rounded = lax.reduce_precision(stats_rows, exponent_bits=8, mantissa_bits=7)
        parts.append(rounded.astype(jnp.bfloat16))
        stats_rows = stats_rows - rounded
    parts = jnp.concatenate(parts, axis=0)
    parts = jnp.pad(parts, ((0, 0), (0, visit_out.shape[1] - rows)))
    ahead = [(s, s + PLANE * far) for s in range(ctx - PLANE * far)]
    got = lax.ppermute(jnp.concatenate([visit_out, parts], axis=0), "ctx", ahead)
    far_out = got[:rows]
    split = visit_stats.shape[1]
    got_parts = got[rows:, :rows].astype(jnp.float32)
    far_stats = (got_parts[:split] + got_parts[split:2 * split] + got_parts[2 * split:]).T

    query_pos = my_index * rows + offsets_in_shard
    near_out, near_stats = partial(
        queries, blocks, key_pos, key_doc, query_pos, docs.reshape(rows, 1), jnp.float32
    )
    has_far = plane >= far
    heads = near_stats.shape[1] // 2
    lane = jnp.arange(2 * heads, dtype=jnp.int32)[None, :]
    far_stats = jnp.where(has_far, far_stats, jnp.where(lane < heads, neg_large, 0.0))
    chunks = merge(near_out, near_stats, far_out, far_stats, out_weight, tp)

    received = lax.all_to_all(chunks, "tp", 0, 0, tiled=True)
    mixed = jnp.sum(received.astype(jnp.float32), axis=0)
    return mixed.astype(jnp.bfloat16)


def solution(mesh):
    placed = (P("ctx", "tp"), P("ctx", "tp"), P("ctx", "tp"), P("ctx"), P("tp", None))
    return jax.shard_map(
        shards, mesh=mesh, in_specs=placed, out_specs=P("ctx", "tp"), check_vma=False
    )
```

```python
import math

import jax
import jax.numpy as jnp
from jax import lax
from jax.experimental import pallas as pl
from jax.experimental.pallas import tpu as pltpu
from jax.sharding import PartitionSpec as P

HEAD_DIM = 128
MAX_DOC = 4224
PLANE = 4
DOC_ROWS = 8
neg_large = -1e30


def partial_kernel(*refs):
    block_ref, key_pos_ref, key_doc_ref = refs[:3]
    sets = len(refs[3:]) // 5
    query_refs = refs[3:3 + sets]
    pos_refs = refs[3 + sets:3 + 2 * sets]
    doc_refs = refs[3 + 2 * sets:3 + 3 * sets]
    out_refs = refs[3 + 3 * sets:3 + 4 * sets]
    stats_refs = refs[3 + 4 * sets:]
    rows = pos_refs[0].shape[0]
    width = out_refs[0].shape[1]
    count, _, packed = block_ref.shape
    head_dim = packed // 2
    heads = width // head_dim
    tokens = count * rows
    key_part = block_ref[:, :rows, :head_dim].reshape(tokens, head_dim)
    value_part = block_ref[:, :rows, head_dim:].reshape(tokens, head_dim)
    key_pos = key_pos_ref[...]
    key_doc = key_doc_ref[...]
    scale = 1.0 / math.sqrt(head_dim)
    for query_ref, pos_ref, doc_ref, out_ref, stats_ref in zip(
        query_refs, pos_refs, doc_refs, out_refs, stats_refs
    ):
        allowed = (key_pos <= pos_ref[...]) & (key_pos >= 0) & (key_doc == doc_ref[...])
        for head in range(heads):
            columns = slice(head * head_dim, (head + 1) * head_dim)
            query = query_ref[:rows, columns]
            scores = lax.dot_general(
                query, key_part, (((1,), (1,)), ((), ())), preferred_element_type=jnp.float32
            )
            scores = scores * scale
            peak = jnp.max(jnp.where(allowed, scores, neg_large), axis=1, keepdims=True)
            weight = jnp.where(allowed, jnp.exp(scores - peak), 0.0)
            total = jnp.sum(weight, axis=1, keepdims=True)
            summed = jnp.dot(
                weight.astype(jnp.bfloat16), value_part, preferred_element_type=jnp.float32
            )
            out_ref[:, columns] = jnp.where(total > 0.0, summed / jnp.maximum(total, 1e-30), 0.0)
            stats_ref[:, head:head + 1] = peak
            stats_ref[:, heads + head:heads + head + 1] = total


def partial(blocks, key_pos, key_doc, queries, positions, docs):
    rows = positions[0].shape[0]
    width = queries[0].shape[1]
    heads = width // HEAD_DIM
    tokens = key_pos.shape[1]
    sets = len(queries)
    vmem = pl.BlockSpec(memory_space=pltpu.VMEM)
    outs = pl.pallas_call(
        partial_kernel,
        out_shape=tuple(
            [jax.ShapeDtypeStruct((rows, width), jnp.float32)] * sets
            + [jax.ShapeDtypeStruct((rows, 2 * heads), jnp.float32)] * sets
        ),
        in_specs=[vmem] * (3 + 3 * sets),
        out_specs=tuple([vmem] * (2 * sets)),
        cost_estimate=pl.CostEstimate(
            flops=4 * sets * rows * tokens * width,
            transcendentals=sets * rows * tokens * heads,
            bytes_accessed=blocks.size * 2 + sets * rows * width * 6,
        ),
    )(blocks, key_pos, key_doc, *queries, *positions, *docs)
    return list(zip(outs[:sets], outs[sets:]))


def combine(first, second):
    out_a, stats_a = first
    out_b, stats_b = second
    rows, width = out_a.shape
    heads = stats_a.shape[1] // 2
    peak = jnp.maximum(stats_a[:, :heads], stats_b[:, :heads])
    share_a = stats_a[:, heads:] * jnp.exp(stats_a[:, :heads] - peak)
    share_b = stats_b[:, heads:] * jnp.exp(stats_b[:, :heads] - peak)
    total = share_a + share_b
    summed = (
        out_a.reshape(rows, heads, -1) * share_a[:, :, None]
        + out_b.astype(jnp.float32).reshape(rows, heads, -1) * share_b[:, :, None]
    )
    out = jnp.where(
        total[:, :, None] > 0.0, summed / jnp.maximum(total, 1e-30)[:, :, None], 0.0
    ).reshape(rows, width)
    return out, jnp.concatenate([peak, total], axis=1)


def pack_rows(out, stats, dtype):
    rows_of = stats.T
    if dtype == jnp.float32:
        parts = rows_of
    else:
        parts = []
        for part in range(3):
            rounded = lax.reduce_precision(rows_of, exponent_bits=8, mantissa_bits=7)
            parts.append(rounded.astype(dtype))
            rows_of = rows_of - rounded
        parts = jnp.concatenate(parts, axis=0)
    parts = jnp.pad(parts.astype(dtype), ((0, 0), (0, out.shape[1] - out.shape[0])))
    return jnp.concatenate([out.astype(dtype), parts], axis=0)


def unpack_rows(packed, rows, split):
    out = packed[:rows]
    parts = packed[rows:, :rows].astype(jnp.float32)
    pieces = parts.shape[0] // split
    stats = parts[:split]
    for piece in range(1, pieces):
        stats = stats + parts[piece * split:(piece + 1) * split]
    return out, stats.T


def merge_kernel(near_ref, near_stats_ref, far_ref, far_stats_ref, weight_ref, out_ref):
    rows, width = near_ref.shape
    heads = near_stats_ref.shape[1] // 2
    head_dim = width // heads
    outputs = []
    for head in range(heads):
        near_peak = near_stats_ref[:, head:head + 1]
        near_total = near_stats_ref[:, heads + head:heads + head + 1]
        far_peak = far_stats_ref[:, head:head + 1]
        far_total = far_stats_ref[:, heads + head:heads + head + 1]
        peak = jnp.maximum(near_peak, far_peak)
        near_share = near_total * jnp.exp(near_peak - peak)
        far_share = far_total * jnp.exp(far_peak - peak)
        columns = slice(head * head_dim, (head + 1) * head_dim)
        summed = (
            near_ref[:, columns].astype(jnp.float32) * near_share
            + far_ref[:, columns].astype(jnp.float32) * far_share
        )
        outputs.append((summed / (near_share + far_share)).astype(jnp.bfloat16))
    attention = jnp.concatenate(outputs, axis=1)
    partial_terms = jnp.dot(attention, weight_ref[...], preferred_element_type=jnp.float32)
    pieces, _, piece_width = out_ref.shape
    for piece in range(pieces):
        out_ref[piece] = partial_terms[:, piece * piece_width:(piece + 1) * piece_width].astype(
            out_ref.dtype
        )


def merge(near, near_stats, far, far_stats, out_weight, pieces):
    rows = near.shape[0]
    width = out_weight.shape[1]
    vmem = pl.BlockSpec(memory_space=pltpu.VMEM)
    return pl.pallas_call(
        merge_kernel,
        out_shape=jax.ShapeDtypeStruct((pieces, rows, width // pieces), jnp.bfloat16),
        in_specs=[vmem] * 5,
        out_specs=vmem,
        cost_estimate=pl.CostEstimate(
            flops=2 * rows * near.shape[1] * width, transcendentals=0,
            bytes_accessed=out_weight.size * 2 + rows * width * 2,
        ),
    )(near, near_stats, far, far_stats, out_weight)


def shards(queries, keys, values, docs, out_weight):
    rows = queries.shape[0]
    head_dim = HEAD_DIM
    heads = queries.shape[1] // head_dim
    ctx = lax.psum(1, "ctx")
    tp = lax.psum(1, "tp")
    my_index = lax.axis_index("ctx")
    plane = my_index // PLANE
    slot = my_index % PLANE
    planes = ctx // PLANE

    shards_back = -(-(MAX_DOC - 1) // rows)
    reach = min(-(-(shards_back + PLANE - 1) // PLANE), planes - 1)
    hops = reach // 2
    far = hops + 1
    step = PLANE * far

    doc_rows = jnp.zeros((DOC_ROWS, 2 * head_dim), jnp.bfloat16)
    doc_rows = doc_rows.at[0, :rows].set(docs.astype(jnp.bfloat16))
    block = jnp.concatenate([jnp.concatenate([keys, values], axis=1), doc_rows], axis=0)

    query_docs = jnp.zeros((DOC_ROWS, queries.shape[1]), jnp.bfloat16)
    query_docs = query_docs.at[0, :rows].set(docs.astype(jnp.bfloat16))
    packed_queries = jnp.concatenate([queries, query_docs], axis=0)
    swap = [(s, s ^ 1) for s in range(ctx)]
    sibling_queries = lax.ppermute(packed_queries, "ctx", swap)
    visit_same = lax.ppermute(packed_queries, "ctx", [(s, s - step) for s in range(step, ctx)])
    visit_other = lax.ppermute(
        packed_queries, "ctx", [(s, (s - step) ^ 1) for s in range(step, ctx)]
    )

    partner = lax.ppermute(block, "ctx", [(s, s ^ 2) for s in range(ctx)])
    current = jnp.stack([block, partner])
    forward = [(s, s + PLANE) for s in range(ctx - PLANE)]
    collected = [current]
    for hop in range(hops):
        current = lax.ppermute(current, "ctx", forward)
        collected.append(current)
    blocks = jnp.stack(collected)

    hop_ids = jnp.arange(hops + 1, dtype=jnp.int32)[:, None, None]
    pair_ids = jnp.arange(2, dtype=jnp.int32)[None, :, None]
    tokens = jnp.arange(rows, dtype=jnp.int32)[None, None, :]
    key_shard = PLANE * (plane - hop_ids) + (slot ^ (2 * pair_ids))
    key_pos = (key_shard * rows + tokens).reshape(1, -1)
    blocks = blocks.reshape(-1, rows + DOC_ROWS, 2 * head_dim)
    key_doc = blocks[:, rows, :rows].astype(jnp.int32).reshape(1, -1)

    offsets_in_shard = jnp.arange(rows, dtype=jnp.int32).reshape(rows, 1)

    def doc_column(packed):
        return packed[rows, :rows].astype(jnp.int32).reshape(rows, 1)

    far_same, far_other = partial(
        blocks, key_pos, key_doc, [visit_same, visit_other],
        [(my_index + step) * rows + offsets_in_shard,
         ((my_index ^ 1) + step) * rows + offsets_in_shard],
        [doc_column(visit_same), doc_column(visit_other)],
    )
    got = lax.ppermute(pack_rows(*far_other, jnp.float32), "ctx", swap)
    far_total = combine(far_same, unpack_rows(got, rows, 2 * heads))
    ahead = [(s, s + step) for s in range(ctx - step)]
    got = lax.ppermute(pack_rows(*far_total, jnp.bfloat16), "ctx", ahead)
    far_out, far_stats = unpack_rows(got, rows, 2 * heads)

    near_own, near_other = partial(
        blocks, key_pos, key_doc, [queries, sibling_queries],
        [my_index * rows + offsets_in_shard, (my_index ^ 1) * rows + offsets_in_shard],
        [docs.reshape(rows, 1), doc_column(sibling_queries)],
    )
    got = lax.ppermute(pack_rows(*near_other, jnp.float32), "ctx", swap)
    near_out, near_stats = combine(near_own, unpack_rows(got, rows, 2 * heads))

    has_far = plane >= far
    lane = jnp.arange(2 * heads, dtype=jnp.int32)[None, :]
    far_stats = jnp.where(has_far, far_stats, jnp.where(lane < heads, neg_large, 0.0))
    chunks = merge(near_out, near_stats, far_out, far_stats, out_weight, tp)

    received = lax.all_to_all(chunks, "tp", 0, 0, tiled=True)
    mixed = jnp.sum(received.astype(jnp.float32), axis=0)
    return mixed.astype(jnp.bfloat16)


def solution(mesh):
    placed = (P("ctx", "tp"), P("ctx", "tp"), P("ctx", "tp"), P("ctx"), P("tp", None))
    return jax.shard_map(
        shards, mesh=mesh, in_specs=placed, out_specs=P("ctx", "tp"), check_vma=False
    )
```

```python
import math

import jax
import jax.numpy as jnp
from jax import lax
from jax.experimental import pallas as pl
from jax.experimental.pallas import tpu as pltpu
from jax.sharding import PartitionSpec as P

HEAD_DIM = 128
MAX_DOC = 4224
PLANE = 4
DOC_ROWS = 8
neg_large = -1e30


def partial_kernel(query_ref, block_ref, key_pos_ref, key_doc_ref, query_pos_ref,
                   query_doc_ref, out_ref, stats_ref):
    rows = query_pos_ref.shape[0]
    width = query_ref.shape[1]
    count, _, packed = block_ref.shape
    head_dim = packed // 2
    heads = width // head_dim
    tokens = count * rows
    key_part = block_ref[:, :rows, :head_dim].reshape(tokens, head_dim)
    value_part = block_ref[:, :rows, head_dim:].reshape(tokens, head_dim)
    allowed = (
        (key_pos_ref[...] <= query_pos_ref[...])
        & (key_pos_ref[...] >= 0)
        & (key_doc_ref[...] == query_doc_ref[...])
    )
    scale = 1.0 / math.sqrt(head_dim)
    for head in range(heads):
        query = query_ref[:rows, head * head_dim:(head + 1) * head_dim]
        scores = lax.dot_general(
            query, key_part, (((1,), (1,)), ((), ())), preferred_element_type=jnp.float32
        )
        scores = scores * scale
        peak = jnp.max(jnp.where(allowed, scores, neg_large), axis=1, keepdims=True)
        weight = jnp.where(allowed, jnp.exp(scores - peak), 0.0)
        total = jnp.sum(weight, axis=1, keepdims=True)
        summed = jnp.dot(
            weight.astype(jnp.bfloat16), value_part, preferred_element_type=jnp.float32
        )
        normed = jnp.where(total > 0.0, summed / jnp.maximum(total, 1e-30), 0.0)
        out_ref[:, head * head_dim:(head + 1) * head_dim] = normed.astype(out_ref.dtype)
        stats_ref[:, head:head + 1] = peak
        stats_ref[:, heads + head:heads + head + 1] = total


def partial(query, blocks, key_pos, key_doc, query_pos, query_doc, out_dtype):
    rows = query_pos.shape[0]
    width = query.shape[1]
    heads = width // HEAD_DIM
    tokens = key_pos.shape[1]
    vmem = pl.BlockSpec(memory_space=pltpu.VMEM)
    return pl.pallas_call(
        partial_kernel,
        out_shape=(
            jax.ShapeDtypeStruct((rows, width), out_dtype),
            jax.ShapeDtypeStruct((rows, 2 * heads), jnp.float32),
        ),
        in_specs=[vmem] * 6,
        out_specs=(vmem, vmem),
        cost_estimate=pl.CostEstimate(
            flops=4 * rows * tokens * width, transcendentals=rows * tokens * heads,
            bytes_accessed=blocks.size * 2 + query.size * 2 + rows * width * 4,
        ),
    )(query, blocks, key_pos, key_doc, query_pos, query_doc)


def merge_kernel(near_ref, near_stats_ref, far_ref, far_stats_ref, weight_ref, out_ref):
    rows, width = near_ref.shape
    heads = near_stats_ref.shape[1] // 2
    head_dim = width // heads
    outputs = []
    for head in range(heads):
        near_peak = near_stats_ref[:, head:head + 1]
        near_total = near_stats_ref[:, heads + head:heads + head + 1]
        far_peak = far_stats_ref[:, head:head + 1]
        far_total = far_stats_ref[:, heads + head:heads + head + 1]
        peak = jnp.maximum(near_peak, far_peak)
        near_share = near_total * jnp.exp(near_peak - peak)
        far_share = far_total * jnp.exp(far_peak - peak)
        columns = slice(head * head_dim, (head + 1) * head_dim)
        summed = (
            near_ref[:, columns].astype(jnp.float32) * near_share
            + far_ref[:, columns].astype(jnp.float32) * far_share
        )
        outputs.append((summed / (near_share + far_share)).astype(jnp.bfloat16))
    attention = jnp.concatenate(outputs, axis=1)
    partial_terms = jnp.dot(attention, weight_ref[...], preferred_element_type=jnp.float32)
    pieces, _, piece_width = out_ref.shape
    for piece in range(pieces):
        out_ref[piece] = partial_terms[:, piece * piece_width:(piece + 1) * piece_width].astype(
            out_ref.dtype
        )


def merge(near, near_stats, far, far_stats, out_weight, pieces):
    rows = near.shape[0]
    width = out_weight.shape[1]
    vmem = pl.BlockSpec(memory_space=pltpu.VMEM)
    return pl.pallas_call(
        merge_kernel,
        out_shape=jax.ShapeDtypeStruct((pieces, rows, width // pieces), jnp.bfloat16),
        in_specs=[vmem] * 5,
        out_specs=vmem,
        cost_estimate=pl.CostEstimate(
            flops=2 * rows * near.shape[1] * width, transcendentals=0,
            bytes_accessed=out_weight.size * 2 + rows * width * 2,
        ),
    )(near, near_stats, far, far_stats, out_weight)


def shards(queries, keys, values, docs, out_weight):
    rows = queries.shape[0]
    head_dim = HEAD_DIM
    ctx = lax.psum(1, "ctx")
    tp = lax.psum(1, "tp")
    my_index = lax.axis_index("ctx")
    plane = my_index // PLANE
    slot = my_index % PLANE
    planes = ctx // PLANE

    shards_back = -(-(MAX_DOC - 1) // rows)
    reach = min(-(-(shards_back + PLANE - 1) // PLANE), planes - 1)
    hops = reach // 2
    far = hops + 1

    doc_rows = jnp.zeros((DOC_ROWS, 2 * head_dim), jnp.bfloat16)
    doc_rows = doc_rows.at[0, :rows].set(docs.astype(jnp.bfloat16))
    block = jnp.concatenate([jnp.concatenate([keys, values], axis=1), doc_rows], axis=0)

    query_docs = jnp.zeros((DOC_ROWS, queries.shape[1]), jnp.bfloat16)
    query_docs = query_docs.at[0, :rows].set(docs.astype(jnp.bfloat16))
    packed_queries = jnp.concatenate([queries, query_docs], axis=0)
    back = [(s, s - PLANE * far) for s in range(PLANE * far, ctx)]

    plane_blocks = [block]
    for offset in range(1, PLANE):
        plane_blocks.append(lax.ppermute(block, "ctx", [(s, s ^ offset) for s in range(ctx)]))
    current = jnp.stack(plane_blocks)
    forward = [(s, s + PLANE) for s in range(ctx - PLANE)]
    collected = [current]
    for hop in range(hops):
        current = lax.ppermute(current, "ctx", forward)
        if hop == 0:
            packed_queries, current = lax.optimization_barrier((packed_queries, current))
            visiting = lax.ppermute(packed_queries, "ctx", back)
        collected.append(current)
    blocks = jnp.stack(collected)

    hop_ids = jnp.arange(hops + 1, dtype=jnp.int32)[:, None, None]
    offsets = jnp.arange(PLANE, dtype=jnp.int32)[None, :, None]
    tokens = jnp.arange(rows, dtype=jnp.int32)[None, None, :]
    key_shard = PLANE * (plane - hop_ids) + (slot ^ offsets)
    key_pos = (key_shard * rows + tokens).reshape(1, -1)
    blocks = blocks.reshape(-1, rows + DOC_ROWS, 2 * head_dim)
    key_doc = blocks[:, rows, :rows].astype(jnp.int32).reshape(1, -1)

    offsets_in_shard = jnp.arange(rows, dtype=jnp.int32).reshape(rows, 1)
    visit_pos = (my_index + PLANE * far) * rows + offsets_in_shard
    visit_doc = visiting[rows, :rows].astype(jnp.int32).reshape(rows, 1)
    visit_out, visit_stats = partial(
        visiting, blocks, key_pos, key_doc, visit_pos, visit_doc, jnp.bfloat16
    )
    ahead = [(s, s + PLANE * far) for s in range(ctx - PLANE * far)]
    far_out = lax.ppermute(visit_out, "ctx", ahead)
    far_stats = lax.ppermute(visit_stats, "ctx", ahead)

    query_pos = my_index * rows + offsets_in_shard
    near_out, near_stats = partial(
        queries, blocks, key_pos, key_doc, query_pos, docs.reshape(rows, 1), jnp.float32
    )
    has_far = plane >= far
    heads = near_stats.shape[1] // 2
    lane = jnp.arange(2 * heads, dtype=jnp.int32)[None, :]
    far_stats = jnp.where(has_far, far_stats, jnp.where(lane < heads, neg_large, 0.0))
    chunks = merge(near_out, near_stats, far_out, far_stats, out_weight, tp)

    received = lax.all_to_all(chunks, "tp", 0, 0, tiled=True)
    mixed = jnp.sum(received.astype(jnp.float32), axis=0)
    return mixed.astype(jnp.bfloat16)


def solution(mesh):
    placed = (P("ctx", "tp"), P("ctx", "tp"), P("ctx", "tp"), P("ctx"), P("tp", None))
    return jax.shard_map(
        shards, mesh=mesh, in_specs=placed, out_specs=P("ctx", "tp"), check_vma=False
    )
```

```python
import math

import jax
import jax.numpy as jnp
from jax import lax
from jax.experimental import pallas as pl
from jax.experimental.pallas import tpu as pltpu
from jax.sharding import PartitionSpec as P

HEAD_DIM = 128
MAX_DOC = 4224
PLANE = 4
DOC_ROWS = 8
neg_large = -1e30


def partial_kernel(*refs):
    query_ref = refs[0]
    block_refs = refs[1:-6]
    key_pos_ref, key_doc_ref, query_pos_ref, query_doc_ref, out_ref, stats_ref = refs[-6:]
    rows = query_pos_ref.shape[0]
    width = query_ref.shape[1]
    head_dim = block_refs[0].shape[-1] // 2
    heads = width // head_dim
    key_part = jnp.concatenate(
        [ref[:, :rows, :head_dim].reshape(ref.shape[0] * rows, head_dim) for ref in block_refs],
        axis=0,
    )
    value_part = jnp.concatenate(
        [ref[:, :rows, head_dim:].reshape(ref.shape[0] * rows, head_dim) for ref in block_refs],
        axis=0,
    )
    allowed = (
        (key_pos_ref[...] <= query_pos_ref[...])
        & (key_pos_ref[...] >= 0)
        & (key_doc_ref[...] == query_doc_ref[...])
    )
    bias = jnp.where(allowed, 0.0, neg_large)
    seen = jnp.max(jnp.where(allowed, 1.0, 0.0), axis=1, keepdims=True) > 0.0
    scale = 1.0 / math.sqrt(head_dim)
    for head in range(heads):
        query = query_ref[:rows, head * head_dim:(head + 1) * head_dim]
        scores = lax.dot_general(
            query, key_part, (((1,), (1,)), ((), ())), preferred_element_type=jnp.float32
        )
        scores = scores * scale + bias
        peak = jnp.max(scores, axis=1, keepdims=True)
        weight = jnp.exp(scores - peak)
        total = jnp.where(seen, jnp.sum(weight, axis=1, keepdims=True), 0.0)
        summed = jnp.dot(
            weight.astype(jnp.bfloat16), value_part, preferred_element_type=jnp.float32
        )
        normed = jnp.where(seen, summed / jnp.maximum(total, 1e-30), 0.0)
        out_ref[:, head * head_dim:(head + 1) * head_dim] = normed.astype(out_ref.dtype)
        stats_ref[:, head:head + 1] = jnp.where(seen, peak, neg_large)
        stats_ref[:, heads + head:heads + head + 1] = total


def partial(query, blocks, key_pos, key_doc, query_pos, query_doc, out_dtype):
    rows = query_pos.shape[0]
    width = query.shape[1]
    heads = width // HEAD_DIM
    tokens = key_pos.shape[1]
    vmem = pl.BlockSpec(memory_space=pltpu.VMEM)
    return pl.pallas_call(
        partial_kernel,
        out_shape=(
            jax.ShapeDtypeStruct((rows, width), out_dtype),
            jax.ShapeDtypeStruct((rows, 2 * heads), jnp.float32),
        ),
        in_specs=[vmem] * (5 + len(blocks)),
        out_specs=(vmem, vmem),
        cost_estimate=pl.CostEstimate(
            flops=4 * rows * tokens * width, transcendentals=rows * tokens * heads,
            bytes_accessed=sum(b.size for b in blocks) * 2 + query.size * 2 + rows * width * 4,
        ),
    )(query, *blocks, key_pos, key_doc, query_pos, query_doc)


def merge_kernel(near_ref, near_stats_ref, far_ref, far_stats_ref, weight_ref, out_ref):
    rows, width = near_ref.shape
    heads = near_stats_ref.shape[1] // 2
    head_dim = width // heads
    outputs = []
    for head in range(heads):
        near_peak = near_stats_ref[:, head:head + 1]
        near_total = near_stats_ref[:, heads + head:heads + head + 1]
        far_peak = far_stats_ref[:, head:head + 1]
        far_total = far_stats_ref[:, heads + head:heads + head + 1]
        peak = jnp.maximum(near_peak, far_peak)
        near_share = near_total * jnp.exp(near_peak - peak)
        far_share = far_total * jnp.exp(far_peak - peak)
        columns = slice(head * head_dim, (head + 1) * head_dim)
        summed = (
            near_ref[:, columns].astype(jnp.float32) * near_share
            + far_ref[:, columns].astype(jnp.float32) * far_share
        )
        outputs.append((summed / (near_share + far_share)).astype(jnp.bfloat16))
    attention = jnp.concatenate(outputs, axis=1)
    partial_terms = jnp.dot(attention, weight_ref[...], preferred_element_type=jnp.float32)
    pieces, _, piece_width = out_ref.shape
    for piece in range(pieces):
        out_ref[piece] = partial_terms[:, piece * piece_width:(piece + 1) * piece_width].astype(
            out_ref.dtype
        )


def merge(near, near_stats, far, far_stats, out_weight, pieces):
    rows = near.shape[0]
    width = out_weight.shape[1]
    vmem = pl.BlockSpec(memory_space=pltpu.VMEM)
    return pl.pallas_call(
        merge_kernel,
        out_shape=jax.ShapeDtypeStruct((pieces, rows, width // pieces), jnp.bfloat16),
        in_specs=[vmem] * 5,
        out_specs=vmem,
        cost_estimate=pl.CostEstimate(
            flops=2 * rows * near.shape[1] * width, transcendentals=0,
            bytes_accessed=out_weight.size * 2 + rows * width * 2,
        ),
    )(near, near_stats, far, far_stats, out_weight)


def shards(queries, keys, values, docs, out_weight):
    rows = queries.shape[0]
    head_dim = HEAD_DIM
    ctx = lax.psum(1, "ctx")
    tp = lax.psum(1, "tp")
    my_index = lax.axis_index("ctx")
    plane = my_index // PLANE
    slot = my_index % PLANE
    planes = ctx // PLANE

    shards_back = -(-(MAX_DOC - 1) // rows)
    reach = min(-(-(shards_back + PLANE - 1) // PLANE), planes - 1)
    hops = reach // 2
    far = hops + 1

    doc_rows = jnp.zeros((DOC_ROWS, 2 * head_dim), jnp.bfloat16)
    doc_rows = doc_rows.at[0, :rows].set(docs.astype(jnp.bfloat16))
    block = jnp.concatenate([jnp.concatenate([keys, values], axis=1), doc_rows], axis=0)

    query_docs = jnp.zeros((DOC_ROWS, queries.shape[1]), jnp.bfloat16)
    query_docs = query_docs.at[0, :rows].set(docs.astype(jnp.bfloat16))
    packed_queries = jnp.concatenate([queries, query_docs], axis=0)
    back = [(s, s - PLANE * far) for s in range(PLANE * far, ctx)]
    visiting = lax.ppermute(packed_queries, "ctx", back)

    plane_blocks = [block]
    for offset in range(1, PLANE):
        plane_blocks.append(lax.ppermute(block, "ctx", [(s, s ^ offset) for s in range(ctx)]))
    current = jnp.stack(plane_blocks)
    forward = [(s, s + PLANE) for s in range(ctx - PLANE)]
    collected = [current]
    for hop in range(hops):
        current = lax.ppermute(current, "ctx", forward)
        collected.append(current)
    blocks = collected

    hop_ids = jnp.arange(hops + 1, dtype=jnp.int32)[:, None, None]
    offsets = jnp.arange(PLANE, dtype=jnp.int32)[None, :, None]
    tokens = jnp.arange(rows, dtype=jnp.int32)[None, None, :]
    key_shard = PLANE * (plane - hop_ids) + (slot ^ offsets)
    key_pos = (key_shard * rows + tokens).reshape(1, -1)
    key_doc = jnp.concatenate(
        [b[:, rows, :rows].astype(jnp.int32).reshape(1, -1) for b in blocks], axis=1
    )

    offsets_in_shard = jnp.arange(rows, dtype=jnp.int32).reshape(rows, 1)
    visit_pos = (my_index + PLANE * far) * rows + offsets_in_shard
    visit_doc = visiting[rows, :rows].astype(jnp.int32).reshape(rows, 1)
    visit_out, visit_stats = partial(
        visiting, blocks, key_pos, key_doc, visit_pos, visit_doc, jnp.bfloat16
    )
    ahead = [(s, s + PLANE * far) for s in range(ctx - PLANE * far)]
    far_out = lax.ppermute(visit_out, "ctx", ahead)
    far_stats = lax.ppermute(visit_stats, "ctx", ahead)

    query_pos = my_index * rows + offsets_in_shard
    near_out, near_stats = partial(
        queries, blocks, key_pos, key_doc, query_pos, docs.reshape(rows, 1), jnp.float32
    )
    has_far = plane >= far
    heads = near_stats.shape[1] // 2
    lane = jnp.arange(2 * heads, dtype=jnp.int32)[None, :]
    far_stats = jnp.where(has_far, far_stats, jnp.where(lane < heads, neg_large, 0.0))
    chunks = merge(near_out, near_stats, far_out, far_stats, out_weight, tp)

    received = lax.all_to_all(chunks, "tp", 0, 0, tiled=True)
    mixed = jnp.sum(received.astype(jnp.float32), axis=0)
    return mixed.astype(jnp.bfloat16)


def solution(mesh):
    placed = (P("ctx", "tp"), P("ctx", "tp"), P("ctx", "tp"), P("ctx"), P("tp", None))
    return jax.shard_map(
        shards, mesh=mesh, in_specs=placed, out_specs=P("ctx", "tp"), check_vma=False
    )
```

```python
import math

import jax
import jax.numpy as jnp
from jax import lax
from jax.experimental import pallas as pl
from jax.experimental.pallas import tpu as pltpu
from jax.sharding import PartitionSpec as P

HEAD_DIM = 128
MAX_DOC = 4224
PLANE = 4
DOC_ROWS = 8
neg_large = -1e30


def partial_kernel(*refs):
    query_ref = refs[0]
    block_refs = refs[1:-8]
    (key_pos_ref, key_doc_ref, query_pos_ref, query_doc_ref, out_ref, stats_ref,
     rows_ref, square_ref) = refs[-8:]
    rows = query_pos_ref.shape[0]
    width = query_ref.shape[1]
    head_dim = block_refs[0].shape[-1] // 2
    heads = width // head_dim
    key_part = jnp.concatenate(
        [ref[:, :rows, :head_dim].reshape(ref.shape[0] * rows, head_dim) for ref in block_refs],
        axis=0,
    )
    value_part = jnp.concatenate(
        [ref[:, :rows, head_dim:].reshape(ref.shape[0] * rows, head_dim) for ref in block_refs],
        axis=0,
    )
    allowed = (
        (key_pos_ref[...] <= query_pos_ref[...])
        & (key_pos_ref[...] >= 0)
        & (key_doc_ref[...] == query_doc_ref[...])
    )
    bias = jnp.where(allowed, 0.0, neg_large)
    seen = jnp.max(jnp.where(allowed, 1.0, 0.0), axis=1, keepdims=True) > 0.0
    scale = 1.0 / math.sqrt(head_dim)
    for head in range(heads):
        query = query_ref[:rows, head * head_dim:(head + 1) * head_dim]
        scores = lax.dot_general(
            query, key_part, (((1,), (1,)), ((), ())), preferred_element_type=jnp.float32
        )
        scores = scores * scale + bias
        peak = jnp.max(scores, axis=1, keepdims=True)
        weight = jnp.exp(scores - peak)
        total = jnp.where(seen, jnp.sum(weight, axis=1, keepdims=True), 0.0)
        summed = jnp.dot(
            weight.astype(jnp.bfloat16), value_part, preferred_element_type=jnp.float32
        )
        normed = jnp.where(seen, summed / jnp.maximum(total, 1e-30), 0.0)
        out_ref[:, head * head_dim:(head + 1) * head_dim] = normed.astype(out_ref.dtype)
        stats_ref[:, head:head + 1] = jnp.where(seen, peak, neg_large)
        stats_ref[:, heads + head:heads + head + 1] = total
    square_ref[...] = jnp.zeros_like(square_ref)
    square_ref[:, :2 * heads] = stats_ref[...]
    rows_ref[...] = jnp.transpose(square_ref[...])[:2 * heads]


def partial(query, blocks, key_pos, key_doc, query_pos, query_doc, out_dtype):
    rows = query_pos.shape[0]
    width = query.shape[1]
    heads = width // HEAD_DIM
    tokens = key_pos.shape[1]
    vmem = pl.BlockSpec(memory_space=pltpu.VMEM)
    return pl.pallas_call(
        partial_kernel,
        out_shape=(
            jax.ShapeDtypeStruct((rows, width), out_dtype),
            jax.ShapeDtypeStruct((rows, 2 * heads), jnp.float32),
            jax.ShapeDtypeStruct((2 * heads, rows), jnp.float32),
        ),
        in_specs=[vmem] * (5 + len(blocks)),
        out_specs=(vmem, vmem, vmem),
        scratch_shapes=[pltpu.VMEM((rows, rows), jnp.float32)],
        cost_estimate=pl.CostEstimate(
            flops=4 * rows * tokens * width, transcendentals=rows * tokens * heads,
            bytes_accessed=sum(b.size for b in blocks) * 2 + query.size * 2 + rows * width * 4,
        ),
    )(query, *blocks, key_pos, key_doc, query_pos, query_doc)


def merge_kernel(near_ref, near_stats_ref, far_ref, far_rows_ref, weight_ref, out_ref,
                 square_ref):
    rows, width = near_ref.shape
    heads = near_stats_ref.shape[1] // 2
    head_dim = width // heads
    square_ref[...] = jnp.zeros_like(square_ref)
    square_ref[:2 * heads, :] = far_rows_ref[...]
    far_stats = jnp.transpose(square_ref[...])
    outputs = []
    for head in range(heads):
        near_peak = near_stats_ref[:, head:head + 1]
        near_total = near_stats_ref[:, heads + head:heads + head + 1]
        far_peak = far_stats[:, head:head + 1]
        far_total = far_stats[:, heads + head:heads + head + 1]
        peak = jnp.maximum(near_peak, far_peak)
        near_share = near_total * jnp.exp(near_peak - peak)
        far_share = far_total * jnp.exp(far_peak - peak)
        columns = slice(head * head_dim, (head + 1) * head_dim)
        summed = (
            near_ref[:, columns].astype(jnp.float32) * near_share
            + far_ref[:, columns].astype(jnp.float32) * far_share
        )
        outputs.append((summed / (near_share + far_share)).astype(jnp.bfloat16))
    attention = jnp.concatenate(outputs, axis=1)
    partial_terms = jnp.dot(attention, weight_ref[...], preferred_element_type=jnp.float32)
    pieces, _, piece_width = out_ref.shape
    for piece in range(pieces):
        out_ref[piece] = partial_terms[:, piece * piece_width:(piece + 1) * piece_width].astype(
            out_ref.dtype
        )


def merge(near, near_stats, far, far_stats, out_weight, pieces):
    rows = near.shape[0]
    width = out_weight.shape[1]
    vmem = pl.BlockSpec(memory_space=pltpu.VMEM)
    return pl.pallas_call(
        merge_kernel,
        out_shape=jax.ShapeDtypeStruct((pieces, rows, width // pieces), jnp.bfloat16),
        in_specs=[vmem] * 5,
        out_specs=vmem,
        scratch_shapes=[pltpu.VMEM((rows, rows), jnp.float32)],
        cost_estimate=pl.CostEstimate(
            flops=2 * rows * near.shape[1] * width, transcendentals=0,
            bytes_accessed=out_weight.size * 2 + rows * width * 2,
        ),
    )(near, near_stats, far, far_stats, out_weight)


def shards(queries, keys, values, docs, out_weight):
    rows = queries.shape[0]
    head_dim = HEAD_DIM
    ctx = lax.psum(1, "ctx")
    tp = lax.psum(1, "tp")
    my_index = lax.axis_index("ctx")
    plane = my_index // PLANE
    slot = my_index % PLANE
    planes = ctx // PLANE

    shards_back = -(-(MAX_DOC - 1) // rows)
    reach = min(-(-(shards_back + PLANE - 1) // PLANE), planes - 1)
    hops = reach // 2
    far = hops + 1

    doc_rows = jnp.zeros((DOC_ROWS, 2 * head_dim), jnp.bfloat16)
    doc_rows = doc_rows.at[0, :rows].set(docs.astype(jnp.bfloat16))
    block = jnp.concatenate([jnp.concatenate([keys, values], axis=1), doc_rows], axis=0)

    query_docs = jnp.zeros((DOC_ROWS, queries.shape[1]), jnp.bfloat16)
    query_docs = query_docs.at[0, :rows].set(docs.astype(jnp.bfloat16))
    packed_queries = jnp.concatenate([queries, query_docs], axis=0)
    back = [(s, s - PLANE * far) for s in range(PLANE * far, ctx)]
    visiting = lax.ppermute(packed_queries, "ctx", back)

    plane_blocks = [block]
    for offset in range(1, PLANE):
        plane_blocks.append(lax.ppermute(block, "ctx", [(s, s ^ offset) for s in range(ctx)]))
    current = jnp.stack(plane_blocks)
    forward = [(s, s + PLANE) for s in range(ctx - PLANE)]
    collected = [current]
    for hop in range(hops):
        current = lax.ppermute(current, "ctx", forward)
        collected.append(current)
    blocks = collected

    hop_ids = jnp.arange(hops + 1, dtype=jnp.int32)[:, None, None]
    offsets = jnp.arange(PLANE, dtype=jnp.int32)[None, :, None]
    tokens = jnp.arange(rows, dtype=jnp.int32)[None, None, :]
    key_shard = PLANE * (plane - hop_ids) + (slot ^ offsets)
    key_pos = (key_shard * rows + tokens).reshape(1, -1)
    key_doc = jnp.concatenate(
        [b[:, rows, :rows].astype(jnp.int32).reshape(1, -1) for b in blocks], axis=1
    )

    offsets_in_shard = jnp.arange(rows, dtype=jnp.int32).reshape(rows, 1)
    visit_pos = (my_index + PLANE * far) * rows + offsets_in_shard
    visit_doc = visiting[rows, :rows].astype(jnp.int32).reshape(rows, 1)
    visit_out, visit_stats, visit_rows = partial(
        visiting, blocks, key_pos, key_doc, visit_pos, visit_doc, jnp.bfloat16
    )
    ahead = [(s, s + PLANE * far) for s in range(ctx - PLANE * far)]
    far_out = lax.ppermute(visit_out, "ctx", ahead)
    far_rows = lax.ppermute(visit_rows, "ctx", ahead)

    query_pos = my_index * rows + offsets_in_shard
    near_out, near_stats, _ = partial(
        queries, blocks, key_pos, key_doc, query_pos, docs.reshape(rows, 1), jnp.float32
    )
    has_far = plane >= far
    heads = near_stats.shape[1] // 2
    kind = jnp.arange(2 * heads, dtype=jnp.int32)[:, None]
    far_rows = jnp.where(has_far, far_rows, jnp.where(kind < heads, neg_large, 0.0))
    chunks = merge(near_out, near_stats, far_out, far_rows, out_weight, tp)

    received = lax.all_to_all(chunks, "tp", 0, 0, tiled=True)
    mixed = jnp.sum(received.astype(jnp.float32), axis=0)
    return mixed.astype(jnp.bfloat16)


def solution(mesh):
    placed = (P("ctx", "tp"), P("ctx", "tp"), P("ctx", "tp"), P("ctx"), P("tp", None))
    return jax.shard_map(
        shards, mesh=mesh, in_specs=placed, out_specs=P("ctx", "tp"), check_vma=False
    )
```

```python
import math

import jax
import jax.numpy as jnp
from jax import lax
from jax.experimental import pallas as pl
from jax.experimental.pallas import tpu as pltpu
from jax.sharding import PartitionSpec as P

HEAD_DIM = 128
MAX_DOC = 4224
PLANE = 4
DOC_ROWS = 8
STAT_ROWS = 32
neg_large = -1e30


def partial_kernel(*refs):
    query_ref = refs[0]
    block_refs = refs[1:-8]
    (key_pos_ref, key_doc_ref, query_pos_ref, query_doc_ref, out_ref, stats_ref,
     rows_ref, square_ref) = refs[-8:]
    rows = query_pos_ref.shape[0]
    width = query_ref.shape[1]
    head_dim = block_refs[0].shape[-1] // 2
    heads = width // head_dim
    key_part = jnp.concatenate(
        [ref[:, :rows, :head_dim].reshape(ref.shape[0] * rows, head_dim) for ref in block_refs],
        axis=0,
    )
    value_part = jnp.concatenate(
        [ref[:, :rows, head_dim:].reshape(ref.shape[0] * rows, head_dim) for ref in block_refs],
        axis=0,
    )
    allowed = (
        (key_pos_ref[...] <= query_pos_ref[...])
        & (key_pos_ref[...] >= 0)
        & (key_doc_ref[...] == query_doc_ref[...])
    )
    bias = jnp.where(allowed, 0.0, neg_large)
    seen = jnp.max(jnp.where(allowed, 1.0, 0.0), axis=1, keepdims=True) > 0.0
    scale = 1.0 / math.sqrt(head_dim)
    for head in range(heads):
        query = query_ref[:rows, head * head_dim:(head + 1) * head_dim]
        scores = lax.dot_general(
            query, key_part, (((1,), (1,)), ((), ())), preferred_element_type=jnp.float32
        )
        scores = scores * scale + bias
        peak = jnp.max(scores, axis=1, keepdims=True)
        weight = jnp.exp(scores - peak)
        total = jnp.where(seen, jnp.sum(weight, axis=1, keepdims=True), 0.0)
        summed = jnp.dot(
            weight.astype(jnp.bfloat16), value_part, preferred_element_type=jnp.float32
        )
        normed = jnp.where(seen, summed / jnp.maximum(total, 1e-30), 0.0)
        out_ref[:rows, head * head_dim:(head + 1) * head_dim] = normed.astype(out_ref.dtype)
        stats_ref[:, head:head + 1] = jnp.where(seen, peak, neg_large)
        stats_ref[:, heads + head:heads + head + 1] = total
    square_ref[...] = jnp.zeros_like(square_ref)
    square_ref[:, :2 * heads] = stats_ref[...]
    stat_rows = jnp.transpose(square_ref[...])[:2 * heads]
    rows_ref[...] = stat_rows
    if out_ref.shape[0] > rows:
        parts = []
        for part in range(3):
            rounded = stat_rows.astype(jnp.bfloat16).astype(jnp.float32)
            parts.append(rounded)
            stat_rows = stat_rows - rounded
        extra = out_ref.shape[0] - rows
        parts.append(jnp.zeros((extra - 6 * heads, rows), jnp.float32))
        out_ref[rows:, :] = jnp.zeros((extra, width), out_ref.dtype)
        out_ref[rows:, :rows] = jnp.concatenate(parts, axis=0).astype(out_ref.dtype)


def partial(query, blocks, key_pos, key_doc, query_pos, query_doc, out_dtype, extra=0):
    rows = query_pos.shape[0]
    width = query.shape[1]
    heads = width // HEAD_DIM
    tokens = key_pos.shape[1]
    vmem = pl.BlockSpec(memory_space=pltpu.VMEM)
    return pl.pallas_call(
        partial_kernel,
        out_shape=(
            jax.ShapeDtypeStruct((rows + extra, width), out_dtype),
            jax.ShapeDtypeStruct((rows, 2 * heads), jnp.float32),
            jax.ShapeDtypeStruct((2 * heads, rows), jnp.float32),
        ),
        in_specs=[vmem] * (5 + len(blocks)),
        out_specs=(vmem, vmem, vmem),
        scratch_shapes=[pltpu.VMEM((rows, rows), jnp.float32)],
        cost_estimate=pl.CostEstimate(
            flops=4 * rows * tokens * width, transcendentals=rows * tokens * heads,
            bytes_accessed=sum(b.size for b in blocks) * 2 + query.size * 2 + rows * width * 4,
        ),
    )(query, *blocks, key_pos, key_doc, query_pos, query_doc)


def merge_kernel(near_ref, near_stats_ref, far_ref, valid_ref, weight_ref, out_ref,
                 square_ref):
    rows, width = near_ref.shape
    heads = near_stats_ref.shape[1] // 2
    head_dim = width // heads
    parts = far_ref[rows:rows + 6 * heads, :rows].astype(jnp.float32)
    stat_rows = parts[:2 * heads] + parts[2 * heads:4 * heads] + parts[4 * heads:]
    kind = lax.broadcasted_iota(jnp.int32, stat_rows.shape, 0)
    valid = valid_ref[...] > 0.0
    fallback = jnp.where(kind < heads, neg_large, 0.0)
    square_ref[...] = jnp.zeros_like(square_ref)
    square_ref[:2 * heads, :] = jnp.where(valid, stat_rows, fallback)
    far_stats = jnp.transpose(square_ref[...])
    outputs = []
    for head in range(heads):
        near_peak = near_stats_ref[:, head:head + 1]
        near_total = near_stats_ref[:, heads + head:heads + head + 1]
        far_peak = far_stats[:, head:head + 1]
        far_total = far_stats[:, heads + head:heads + head + 1]
        peak = jnp.maximum(near_peak, far_peak)
        near_share = near_total * jnp.exp(near_peak - peak)
        far_share = far_total * jnp.exp(far_peak - peak)
        columns = slice(head * head_dim, (head + 1) * head_dim)
        far_part = jnp.where(valid[:, :1], far_ref[:rows, columns].astype(jnp.float32), 0.0)
        summed = near_ref[:, columns].astype(jnp.float32) * near_share + far_part * far_share
        outputs.append((summed / (near_share + far_share)).astype(jnp.bfloat16))
    attention = jnp.concatenate(outputs, axis=1)
    partial_terms = jnp.dot(attention, weight_ref[...], preferred_element_type=jnp.float32)
    pieces, _, piece_width = out_ref.shape
    for piece in range(pieces):
        out_ref[piece] = partial_terms[:, piece * piece_width:(piece + 1) * piece_width].astype(
            out_ref.dtype
        )


def merge(near, near_stats, far, far_stats, out_weight, pieces):
    rows = near.shape[0]
    width = out_weight.shape[1]
    vmem = pl.BlockSpec(memory_space=pltpu.VMEM)
    return pl.pallas_call(
        merge_kernel,
        out_shape=jax.ShapeDtypeStruct((pieces, rows, width // pieces), jnp.bfloat16),
        in_specs=[vmem] * 5,
        out_specs=vmem,
        scratch_shapes=[pltpu.VMEM((rows, rows), jnp.float32)],
        cost_estimate=pl.CostEstimate(
            flops=2 * rows * near.shape[1] * width, transcendentals=0,
            bytes_accessed=out_weight.size * 2 + rows * width * 2,
        ),
    )(near, near_stats, far, far_stats, out_weight)


def shards(queries, keys, values, docs, out_weight):
    rows = queries.shape[0]
    head_dim = HEAD_DIM
    ctx = lax.psum(1, "ctx")
    tp = lax.psum(1, "tp")
    my_index = lax.axis_index("ctx")
    plane = my_index // PLANE
    slot = my_index % PLANE
    planes = ctx // PLANE

    shards_back = -(-(MAX_DOC - 1) // rows)
    reach = min(-(-(shards_back + PLANE - 1) // PLANE), planes - 1)
    hops = reach // 2
    far = hops + 1

    doc_rows = jnp.zeros((DOC_ROWS, 2 * head_dim), jnp.bfloat16)
    doc_rows = doc_rows.at[0, :rows].set(docs.astype(jnp.bfloat16))
    block = jnp.concatenate([jnp.concatenate([keys, values], axis=1), doc_rows], axis=0)

    query_docs = jnp.zeros((DOC_ROWS, queries.shape[1]), jnp.bfloat16)
    query_docs = query_docs.at[0, :rows].set(docs.astype(jnp.bfloat16))
    packed_queries = jnp.concatenate([queries, query_docs], axis=0)
    back = [(s, s - PLANE * far) for s in range(PLANE * far, ctx)]
    visiting = lax.ppermute(packed_queries, "ctx", back)

    plane_blocks = [block]
    for offset in range(1, PLANE):
        plane_blocks.append(lax.ppermute(block, "ctx", [(s, s ^ offset) for s in range(ctx)]))
    current = jnp.stack(plane_blocks)
    forward = [(s, s + PLANE) for s in range(ctx - PLANE)]
    collected = [current]
    for hop in range(hops):
        current = lax.ppermute(current, "ctx", forward)
        collected.append(current)
    blocks = collected

    hop_ids = jnp.arange(hops + 1, dtype=jnp.int32)[:, None, None]
    offsets = jnp.arange(PLANE, dtype=jnp.int32)[None, :, None]
    tokens = jnp.arange(rows, dtype=jnp.int32)[None, None, :]
    key_shard = PLANE * (plane - hop_ids) + (slot ^ offsets)
    key_pos = (key_shard * rows + tokens).reshape(1, -1)
    key_doc = jnp.concatenate(
        [b[:, rows, :rows].astype(jnp.int32).reshape(1, -1) for b in blocks], axis=1
    )

    offsets_in_shard = jnp.arange(rows, dtype=jnp.int32).reshape(rows, 1)
    visit_pos = (my_index + PLANE * far) * rows + offsets_in_shard
    visit_doc = visiting[rows, :rows].astype(jnp.int32).reshape(rows, 1)
    visit_out, visit_stats, visit_rows = partial(
        visiting, blocks, key_pos, key_doc, visit_pos, visit_doc, jnp.bfloat16, STAT_ROWS
    )
    ahead = [(s, s + PLANE * far) for s in range(ctx - PLANE * far)]
    far_out = lax.ppermute(visit_out, "ctx", ahead)

    query_pos = my_index * rows + offsets_in_shard
    near_out, near_stats, _ = partial(
        queries, blocks, key_pos, key_doc, query_pos, docs.reshape(rows, 1), jnp.float32
    )
    has_far = plane >= far
    heads = near_stats.shape[1] // 2
    valid = jnp.where(has_far, 1.0, 0.0) * jnp.ones((1, rows), jnp.float32)
    chunks = merge(near_out, near_stats, far_out, valid, out_weight, tp)

    received = lax.all_to_all(chunks, "tp", 0, 0, tiled=True)
    mixed = jnp.sum(received.astype(jnp.float32), axis=0)
    return mixed.astype(jnp.bfloat16)


def solution(mesh):
    placed = (P("ctx", "tp"), P("ctx", "tp"), P("ctx", "tp"), P("ctx"), P("tp", None))
    return jax.shard_map(
        shards, mesh=mesh, in_specs=placed, out_specs=P("ctx", "tp"), check_vma=False
    )
```

```python
import math

import jax
import jax.numpy as jnp
from jax import lax
from jax.experimental import pallas as pl
from jax.experimental.pallas import tpu as pltpu
from jax.sharding import PartitionSpec as P

HEAD_DIM = 128
MAX_DOC = 4224
PLANE = 4
DOC_ROWS = 8
neg_large = -1e30


def partial_kernel(*refs):
    query_ref = refs[0]
    block_refs = refs[1:-8]
    (key_pos_ref, key_doc_ref, query_pos_ref, query_doc_ref, out_ref, stats_ref,
     rows_ref, square_ref) = refs[-8:]
    rows = query_pos_ref.shape[0]
    width = query_ref.shape[1]
    head_dim = block_refs[0].shape[-1] // 2
    heads = width // head_dim
    key_part = jnp.concatenate(
        [ref[:, :rows, :head_dim].reshape(ref.shape[0] * rows, head_dim) for ref in block_refs],
        axis=0,
    )
    value_part = jnp.concatenate(
        [ref[:, :rows, head_dim:].reshape(ref.shape[0] * rows, head_dim) for ref in block_refs],
        axis=0,
    )
    allowed = (
        (key_pos_ref[...] <= query_pos_ref[...])
        & (key_pos_ref[...] >= 0)
        & (key_doc_ref[...] == query_doc_ref[...])
    )
    bias = jnp.where(allowed, 0.0, neg_large)
    seen = jnp.max(jnp.where(allowed, 1.0, 0.0), axis=1, keepdims=True) > 0.0
    scale = 1.0 / math.sqrt(head_dim)
    for head in range(heads):
        query = query_ref[:rows, head * head_dim:(head + 1) * head_dim]
        scores = lax.dot_general(
            query, key_part, (((1,), (1,)), ((), ())), preferred_element_type=jnp.float32
        )
        scores = scores * scale + bias
        peak = jnp.max(scores, axis=1, keepdims=True)
        weight = jnp.exp(scores - peak)
        total = jnp.where(seen, jnp.sum(weight, axis=1, keepdims=True), 0.0)
        summed = jnp.dot(
            weight.astype(jnp.bfloat16), value_part, preferred_element_type=jnp.float32
        )
        normed = jnp.where(seen, summed / jnp.maximum(total, 1e-30), 0.0)
        out_ref[:, head * head_dim:(head + 1) * head_dim] = normed.astype(out_ref.dtype)
        stats_ref[:, head:head + 1] = jnp.where(seen, peak, neg_large)
        stats_ref[:, heads + head:heads + head + 1] = total
    square_ref[...] = jnp.zeros_like(square_ref)
    square_ref[:, :2 * heads] = stats_ref[...]
    rows_ref[...] = jnp.transpose(square_ref[...])[:2 * heads]


def partial(query, blocks, key_pos, key_doc, query_pos, query_doc, out_dtype):
    rows = query_pos.shape[0]
    width = query.shape[1]
    heads = width // HEAD_DIM
    tokens = key_pos.shape[1]
    vmem = pl.BlockSpec(memory_space=pltpu.VMEM)
    return pl.pallas_call(
        partial_kernel,
        out_shape=(
            jax.ShapeDtypeStruct((rows, width), out_dtype),
            jax.ShapeDtypeStruct((rows, 2 * heads), jnp.float32),
            jax.ShapeDtypeStruct((2 * heads, rows), jnp.float32),
        ),
        in_specs=[vmem] * (5 + len(blocks)),
        out_specs=(vmem, vmem, vmem),
        scratch_shapes=[pltpu.VMEM((rows, rows), jnp.float32)],
        cost_estimate=pl.CostEstimate(
            flops=4 * rows * tokens * width, transcendentals=rows * tokens * heads,
            bytes_accessed=sum(b.size for b in blocks) * 2 + query.size * 2 + rows * width * 4,
        ),
    )(query, *blocks, key_pos, key_doc, query_pos, query_doc)


def merge_kernel(near_ref, near_stats_ref, far_ref, far_rows_ref, weight_ref, out_ref,
                 square_ref):
    rows, width = near_ref.shape
    heads = near_stats_ref.shape[1] // 2
    head_dim = width // heads
    square_ref[...] = jnp.zeros_like(square_ref)
    square_ref[:2 * heads, :] = far_rows_ref[...]
    far_stats = jnp.transpose(square_ref[...])
    outputs = []
    for head in range(heads):
        near_peak = near_stats_ref[:, head:head + 1]
        near_total = near_stats_ref[:, heads + head:heads + head + 1]
        far_peak = far_stats[:, head:head + 1]
        far_total = far_stats[:, heads + head:heads + head + 1]
        peak = jnp.maximum(near_peak, far_peak)
        near_share = near_total * jnp.exp(near_peak - peak)
        far_share = far_total * jnp.exp(far_peak - peak)
        columns = slice(head * head_dim, (head + 1) * head_dim)
        summed = (
            near_ref[:, columns].astype(jnp.float32) * near_share
            + far_ref[:, columns].astype(jnp.float32) * far_share
        )
        outputs.append((summed / (near_share + far_share)).astype(jnp.bfloat16))
    attention = jnp.concatenate(outputs, axis=1)
    partial_terms = jnp.dot(attention, weight_ref[...], preferred_element_type=jnp.float32)
    pieces, _, piece_width = out_ref.shape
    for piece in range(pieces):
        out_ref[piece] = partial_terms[:, piece * piece_width:(piece + 1) * piece_width].astype(
            out_ref.dtype
        )


def merge(near, near_stats, far, far_stats, out_weight, pieces):
    rows = near.shape[0]
    width = out_weight.shape[1]
    vmem = pl.BlockSpec(memory_space=pltpu.VMEM)
    return pl.pallas_call(
        merge_kernel,
        out_shape=jax.ShapeDtypeStruct((pieces, rows, width // pieces), jnp.bfloat16),
        in_specs=[vmem] * 5,
        out_specs=vmem,
        scratch_shapes=[pltpu.VMEM((rows, rows), jnp.float32)],
        cost_estimate=pl.CostEstimate(
            flops=2 * rows * near.shape[1] * width, transcendentals=0,
            bytes_accessed=out_weight.size * 2 + rows * width * 2,
        ),
    )(near, near_stats, far, far_stats, out_weight)


def shards(queries, keys, values, docs, out_weight):
    rows = queries.shape[0]
    head_dim = HEAD_DIM
    ctx = lax.psum(1, "ctx")
    tp = lax.psum(1, "tp")
    my_index = lax.axis_index("ctx")
    plane = my_index // PLANE
    slot = my_index % PLANE
    planes = ctx // PLANE

    shards_back = -(-(MAX_DOC - 1) // rows)
    reach = min(-(-(shards_back + PLANE - 1) // PLANE), planes - 1)
    hops = (reach + 1) // 2
    far_planes = reach - hops
    far = hops + 1

    doc_rows = jnp.zeros((DOC_ROWS, 2 * head_dim), jnp.bfloat16)
    doc_rows = doc_rows.at[0, :rows].set(docs.astype(jnp.bfloat16))
    block = jnp.concatenate([jnp.concatenate([keys, values], axis=1), doc_rows], axis=0)

    query_docs = jnp.zeros((DOC_ROWS, queries.shape[1]), jnp.bfloat16)
    query_docs = query_docs.at[0, :rows].set(docs.astype(jnp.bfloat16))
    packed_queries = jnp.concatenate([queries, query_docs], axis=0)
    back = [(s, s - PLANE * far) for s in range(PLANE * far, ctx)]
    visiting = lax.ppermute(packed_queries, "ctx", back)

    plane_blocks = [block]
    for offset in range(1, PLANE):
        plane_blocks.append(lax.ppermute(block, "ctx", [(s, s ^ offset) for s in range(ctx)]))
    current = jnp.stack(plane_blocks)
    forward = [(s, s + PLANE) for s in range(ctx - PLANE)]
    collected = [current]
    for hop in range(hops):
        current = lax.ppermute(current, "ctx", forward)
        collected.append(current)
    blocks = collected

    hop_ids = jnp.arange(hops + 1, dtype=jnp.int32)[:, None, None]
    offsets = jnp.arange(PLANE, dtype=jnp.int32)[None, :, None]
    tokens = jnp.arange(rows, dtype=jnp.int32)[None, None, :]
    key_shard = PLANE * (plane - hop_ids) + (slot ^ offsets)
    key_pos = (key_shard * rows + tokens).reshape(hops + 1, -1)
    key_doc = [b[:, rows, :rows].astype(jnp.int32).reshape(1, -1) for b in blocks]
    far_blocks = blocks[:far_planes]
    far_key_pos = key_pos[:far_planes].reshape(1, -1)
    far_key_doc = jnp.concatenate(key_doc[:far_planes], axis=1)
    key_pos = key_pos.reshape(1, -1)
    key_doc = jnp.concatenate(key_doc, axis=1)

    offsets_in_shard = jnp.arange(rows, dtype=jnp.int32).reshape(rows, 1)
    visit_pos = (my_index + PLANE * far) * rows + offsets_in_shard
    visit_doc = visiting[rows, :rows].astype(jnp.int32).reshape(rows, 1)
    visit_out, visit_stats, visit_rows = partial(
        visiting, far_blocks, far_key_pos, far_key_doc, visit_pos, visit_doc, jnp.bfloat16
    )
    ahead = [(s, s + PLANE * far) for s in range(ctx - PLANE * far)]
    far_out = lax.ppermute(visit_out, "ctx", ahead)
    far_rows = lax.ppermute(visit_rows, "ctx", ahead)

    query_pos = my_index * rows + offsets_in_shard
    near_out, near_stats, _ = partial(
        queries, blocks, key_pos, key_doc, query_pos, docs.reshape(rows, 1), jnp.float32
    )
    has_far = plane >= far
    heads = near_stats.shape[1] // 2
    kind = jnp.arange(2 * heads, dtype=jnp.int32)[:, None]
    far_rows = jnp.where(has_far, far_rows, jnp.where(kind < heads, neg_large, 0.0))
    chunks = merge(near_out, near_stats, far_out, far_rows, out_weight, tp)

    received = lax.all_to_all(chunks, "tp", 0, 0, tiled=True)
    mixed = jnp.sum(received.astype(jnp.float32), axis=0)
    return mixed.astype(jnp.bfloat16)


def solution(mesh):
    placed = (P("ctx", "tp"), P("ctx", "tp"), P("ctx", "tp"), P("ctx"), P("tp", None))
    return jax.shard_map(
        shards, mesh=mesh, in_specs=placed, out_specs=P("ctx", "tp"), check_vma=False
    )
```

```python
import math

import jax
import jax.numpy as jnp
from jax import lax
from jax.experimental import pallas as pl
from jax.experimental.pallas import tpu as pltpu
from jax.sharding import PartitionSpec as P

HEAD_DIM = 128
MAX_DOC = 4224
PLANE = 4
DOC_ROWS = 8
neg_large = -1e30


def partial_kernel(*refs):
    query_ref = refs[0]
    block_refs = refs[1:-8]
    (key_pos_ref, key_doc_ref, query_pos_ref, query_doc_ref, out_ref, stats_ref,
     rows_ref, square_ref) = refs[-8:]
    rows = query_pos_ref.shape[0]
    width = query_ref.shape[1]
    head_dim = block_refs[0].shape[-1] // 2
    heads = width // head_dim
    key_part = jnp.concatenate(
        [ref[:, :rows, :head_dim].reshape(ref.shape[0] * rows, head_dim) for ref in block_refs],
        axis=0,
    )
    value_part = jnp.concatenate(
        [ref[:, :rows, head_dim:].reshape(ref.shape[0] * rows, head_dim) for ref in block_refs],
        axis=0,
    )
    allowed = (
        (key_pos_ref[...] <= query_pos_ref[...])
        & (key_pos_ref[...] >= 0)
        & (key_doc_ref[...] == query_doc_ref[...])
    )
    bias = jnp.where(allowed, 0.0, neg_large)
    seen = jnp.max(jnp.where(allowed, 1.0, 0.0), axis=1, keepdims=True) > 0.0
    scale = 1.0 / math.sqrt(head_dim)
    for head in range(heads):
        query = query_ref[:rows, head * head_dim:(head + 1) * head_dim]
        scores = lax.dot_general(
            query, key_part, (((1,), (1,)), ((), ())), preferred_element_type=jnp.float32
        )
        scores = scores * scale + bias
        peak = jnp.max(scores, axis=1, keepdims=True)
        weight = jnp.exp(scores - peak)
        total = jnp.where(seen, jnp.sum(weight, axis=1, keepdims=True), 0.0)
        summed = jnp.dot(
            weight.astype(jnp.bfloat16), value_part, preferred_element_type=jnp.float32
        )
        normed = jnp.where(seen, summed / jnp.maximum(total, 1e-30), 0.0)
        out_ref[:, head * head_dim:(head + 1) * head_dim] = normed.astype(out_ref.dtype)
        stats_ref[:, head:head + 1] = jnp.where(seen, peak, neg_large)
        stats_ref[:, heads + head:heads + head + 1] = total
    square_ref[...] = jnp.zeros_like(square_ref)
    square_ref[:, :2 * heads] = stats_ref[...]
    rows_ref[...] = jnp.transpose(square_ref[...])[:2 * heads]


def partial(query, blocks, key_pos, key_doc, query_pos, query_doc, out_dtype):
    rows = query_pos.shape[0]
    width = query.shape[1]
    heads = width // HEAD_DIM
    tokens = key_pos.shape[1]
    vmem = pl.BlockSpec(memory_space=pltpu.VMEM)
    return pl.pallas_call(
        partial_kernel,
        out_shape=(
            jax.ShapeDtypeStruct((rows, width), out_dtype),
            jax.ShapeDtypeStruct((rows, 2 * heads), jnp.float32),
            jax.ShapeDtypeStruct((2 * heads, rows), jnp.float32),
        ),
        in_specs=[vmem] * (5 + len(blocks)),
        out_specs=(vmem, vmem, vmem),
        scratch_shapes=[pltpu.VMEM((rows, rows), jnp.float32)],
        cost_estimate=pl.CostEstimate(
            flops=4 * rows * tokens * width, transcendentals=rows * tokens * heads,
            bytes_accessed=sum(b.size for b in blocks) * 2 + query.size * 2 + rows * width * 4,
        ),
    )(query, *blocks, key_pos, key_doc, query_pos, query_doc)


def merge_kernel(near_ref, near_stats_ref, far_ref, far_rows_ref, weight_ref, out_ref,
                 square_ref):
    rows, width = near_ref.shape
    heads = near_stats_ref.shape[1] // 2
    head_dim = width // heads
    square_ref[...] = jnp.zeros_like(square_ref)
    square_ref[:2 * heads, :] = far_rows_ref[...]
    far_stats = jnp.transpose(square_ref[...])
    outputs = []
    for head in range(heads):
        near_peak = near_stats_ref[:, head:head + 1]
        near_total = near_stats_ref[:, heads + head:heads + head + 1]
        far_peak = far_stats[:, head:head + 1]
        far_total = far_stats[:, heads + head:heads + head + 1]
        peak = jnp.maximum(near_peak, far_peak)
        near_share = near_total * jnp.exp(near_peak - peak)
        far_share = far_total * jnp.exp(far_peak - peak)
        columns = slice(head * head_dim, (head + 1) * head_dim)
        summed = (
            near_ref[:, columns].astype(jnp.float32) * near_share
            + far_ref[:, columns].astype(jnp.float32) * far_share
        )
        outputs.append((summed / (near_share + far_share)).astype(jnp.bfloat16))
    attention = jnp.concatenate(outputs, axis=1)
    partial_terms = jnp.dot(attention, weight_ref[...], preferred_element_type=jnp.float32)
    pieces, _, piece_width = out_ref.shape
    for piece in range(pieces):
        out_ref[piece] = partial_terms[:, piece * piece_width:(piece + 1) * piece_width].astype(
            out_ref.dtype
        )


def merge(near, near_stats, far, far_stats, out_weight, pieces):
    rows = near.shape[0]
    width = out_weight.shape[1]
    vmem = pl.BlockSpec(memory_space=pltpu.VMEM)
    return pl.pallas_call(
        merge_kernel,
        out_shape=jax.ShapeDtypeStruct((pieces, rows, width // pieces), jnp.bfloat16),
        in_specs=[vmem] * 5,
        out_specs=vmem,
        scratch_shapes=[pltpu.VMEM((rows, rows), jnp.float32)],
        cost_estimate=pl.CostEstimate(
            flops=2 * rows * near.shape[1] * width, transcendentals=0,
            bytes_accessed=out_weight.size * 2 + rows * width * 2,
        ),
    )(near, near_stats, far, far_stats, out_weight)


def shards(queries, keys, values, docs, out_weight):
    rows = queries.shape[0]
    head_dim = HEAD_DIM
    ctx = lax.psum(1, "ctx")
    tp = lax.psum(1, "tp")
    my_index = lax.axis_index("ctx")
    plane = my_index // PLANE
    slot = my_index % PLANE
    planes = ctx // PLANE

    shards_back = -(-(MAX_DOC - 1) // rows)
    reach = min(-(-(shards_back + PLANE - 1) // PLANE), planes - 1)
    hops = reach // 2
    far = hops + 1

    doc_rows = jnp.zeros((DOC_ROWS, 2 * head_dim), jnp.bfloat16)
    doc_rows = doc_rows.at[0, :rows].set(docs.astype(jnp.bfloat16))
    block = jnp.concatenate([jnp.concatenate([keys, values], axis=1), doc_rows], axis=0)

    query_docs = jnp.zeros((DOC_ROWS, queries.shape[1]), jnp.bfloat16)
    query_docs = query_docs.at[0, :rows].set(docs.astype(jnp.bfloat16))
    packed_queries = jnp.concatenate([queries, query_docs], axis=0)
    back = [(s, s - PLANE * far) for s in range(PLANE * far, ctx)]
    visiting = lax.ppermute(packed_queries, "ctx", back)

    plane_blocks = [block]
    for offset in range(1, PLANE):
        plane_blocks.append(lax.ppermute(block, "ctx", [(s, s ^ offset) for s in range(ctx)]))
    current = jnp.stack(plane_blocks)
    forward = [(s, s + PLANE) for s in range(ctx - PLANE)]
    collected = [current]
    for hop in range(hops):
        current = lax.ppermute(current, "ctx", forward)
        collected.append(current)
    blocks = collected

    hop_ids = jnp.arange(hops + 1, dtype=jnp.int32)[:, None, None]
    offsets = jnp.arange(PLANE, dtype=jnp.int32)[None, :, None]
    tokens = jnp.arange(rows, dtype=jnp.int32)[None, None, :]
    key_shard = PLANE * (plane - hop_ids) + (slot ^ offsets)
    key_pos = (key_shard * rows + tokens).reshape(1, -1)
    key_doc = jnp.concatenate(
        [b[:, rows, :rows].astype(jnp.int32).reshape(1, -1) for b in blocks], axis=1
    )

    offsets_in_shard = jnp.arange(rows, dtype=jnp.int32).reshape(rows, 1)
    visit_pos = (my_index + PLANE * far) * rows + offsets_in_shard
    visit_doc = visiting[rows, :rows].astype(jnp.int32).reshape(rows, 1)
    visit_out, visit_stats, visit_rows = partial(
        visiting, blocks, key_pos, key_doc, visit_pos, visit_doc, jnp.bfloat16
    )
    query_pos = my_index * rows + offsets_in_shard
    near_out, near_stats, _ = partial(
        queries, blocks, key_pos, key_doc, query_pos, docs.reshape(rows, 1), jnp.float32
    )
    visit_out, visit_rows, near_out, near_stats = lax.optimization_barrier(
        (visit_out, visit_rows, near_out, near_stats)
    )
    ahead = [(s, s + PLANE * far) for s in range(ctx - PLANE * far)]
    far_out = lax.ppermute(visit_out, "ctx", ahead)
    far_rows = lax.ppermute(visit_rows, "ctx", ahead)
    has_far = plane >= far
    heads = near_stats.shape[1] // 2
    kind = jnp.arange(2 * heads, dtype=jnp.int32)[:, None]
    far_rows = jnp.where(has_far, far_rows, jnp.where(kind < heads, neg_large, 0.0))
    chunks = merge(near_out, near_stats, far_out, far_rows, out_weight, tp)

    received = lax.all_to_all(chunks, "tp", 0, 0, tiled=True)
    mixed = jnp.sum(received.astype(jnp.float32), axis=0)
    return mixed.astype(jnp.bfloat16)


def solution(mesh):
    placed = (P("ctx", "tp"), P("ctx", "tp"), P("ctx", "tp"), P("ctx"), P("tp", None))
    return jax.shard_map(
        shards, mesh=mesh, in_specs=placed, out_specs=P("ctx", "tp"), check_vma=False
    )
```

```python
import math

import jax
import jax.numpy as jnp
from jax import lax
from jax.experimental import pallas as pl
from jax.experimental.pallas import tpu as pltpu
from jax.sharding import PartitionSpec as P

HEAD_DIM = 128
MAX_DOC = 4224
PLANE = 4
DOC_ROWS = 8
neg_large = -1e30


def partial_kernel(*refs):
    query_ref = refs[0]
    block_refs = refs[1:-8]
    (key_pos_ref, key_doc_ref, query_pos_ref, query_doc_ref, out_ref, stats_ref,
     rows_ref, square_ref) = refs[-8:]
    rows = query_pos_ref.shape[0]
    width = query_ref.shape[1]
    head_dim = block_refs[0].shape[-1] // 2
    heads = width // head_dim
    key_part = jnp.concatenate(
        [ref[:, :rows, :head_dim].reshape(ref.shape[0] * rows, head_dim) for ref in block_refs],
        axis=0,
    )
    value_part = jnp.concatenate(
        [ref[:, :rows, head_dim:].reshape(ref.shape[0] * rows, head_dim) for ref in block_refs],
        axis=0,
    )
    allowed = (
        (key_pos_ref[...] <= query_pos_ref[...])
        & (key_pos_ref[...] >= 0)
        & (key_doc_ref[...] == query_doc_ref[...])
    )
    bias = jnp.where(allowed, 0.0, neg_large)
    seen = jnp.max(jnp.where(allowed, 1.0, 0.0), axis=1, keepdims=True) > 0.0
    scale = 1.0 / math.sqrt(head_dim)
    query = jnp.concatenate(
        [query_ref[:rows, head * head_dim:(head + 1) * head_dim] for head in range(heads)],
        axis=0,
    )
    scores = lax.dot_general(
        query, key_part, (((1,), (1,)), ((), ())), preferred_element_type=jnp.float32
    )
    scores = scores.reshape(heads, rows, -1) * scale + bias[None]
    peak = jnp.max(scores, axis=2, keepdims=True)
    weight = jnp.exp(scores - peak)
    total = jnp.where(seen[None], jnp.sum(weight, axis=2, keepdims=True), 0.0)
    summed = jnp.dot(
        weight.reshape(heads * rows, -1).astype(jnp.bfloat16), value_part,
        preferred_element_type=jnp.float32,
    ).reshape(heads, rows, head_dim)
    for head in range(heads):
        normed = jnp.where(seen, summed[head] / jnp.maximum(total[head], 1e-30), 0.0)
        out_ref[:, head * head_dim:(head + 1) * head_dim] = normed.astype(out_ref.dtype)
        stats_ref[:, head:head + 1] = jnp.where(seen, peak[head], neg_large)
        stats_ref[:, heads + head:heads + head + 1] = total[head]
    square_ref[...] = jnp.zeros_like(square_ref)
    square_ref[:, :2 * heads] = stats_ref[...]
    rows_ref[...] = jnp.transpose(square_ref[...])[:2 * heads]


def partial(query, blocks, key_pos, key_doc, query_pos, query_doc, out_dtype):
    rows = query_pos.shape[0]
    width = query.shape[1]
    heads = width // HEAD_DIM
    tokens = key_pos.shape[1]
    vmem = pl.BlockSpec(memory_space=pltpu.VMEM)
    return pl.pallas_call(
        partial_kernel,
        out_shape=(
            jax.ShapeDtypeStruct((rows, width), out_dtype),
            jax.ShapeDtypeStruct((rows, 2 * heads), jnp.float32),
            jax.ShapeDtypeStruct((2 * heads, rows), jnp.float32),
        ),
        in_specs=[vmem] * (5 + len(blocks)),
        out_specs=(vmem, vmem, vmem),
        scratch_shapes=[pltpu.VMEM((rows, rows), jnp.float32)],
        cost_estimate=pl.CostEstimate(
            flops=4 * rows * tokens * width, transcendentals=rows * tokens * heads,
            bytes_accessed=sum(b.size for b in blocks) * 2 + query.size * 2 + rows * width * 4,
        ),
    )(query, *blocks, key_pos, key_doc, query_pos, query_doc)


def merge_kernel(near_ref, near_stats_ref, far_ref, far_rows_ref, weight_ref, out_ref,
                 square_ref):
    rows, width = near_ref.shape
    heads = near_stats_ref.shape[1] // 2
    head_dim = width // heads
    square_ref[...] = jnp.zeros_like(square_ref)
    square_ref[:2 * heads, :] = far_rows_ref[...]
    far_stats = jnp.transpose(square_ref[...])
    outputs = []
    for head in range(heads):
        near_peak = near_stats_ref[:, head:head + 1]
        near_total = near_stats_ref[:, heads + head:heads + head + 1]
        far_peak = far_stats[:, head:head + 1]
        far_total = far_stats[:, heads + head:heads + head + 1]
        peak = jnp.maximum(near_peak, far_peak)
        near_share = near_total * jnp.exp(near_peak - peak)
        far_share = far_total * jnp.exp(far_peak - peak)
        columns = slice(head * head_dim, (head + 1) * head_dim)
        summed = (
            near_ref[:, columns].astype(jnp.float32) * near_share
            + far_ref[:, columns].astype(jnp.float32) * far_share
        )
        outputs.append((summed / (near_share + far_share)).astype(jnp.bfloat16))
    attention = jnp.concatenate(outputs, axis=1)
    partial_terms = jnp.dot(attention, weight_ref[...], preferred_element_type=jnp.float32)
    pieces, _, piece_width = out_ref.shape
    for piece in range(pieces):
        out_ref[piece] = partial_terms[:, piece * piece_width:(piece + 1) * piece_width].astype(
            out_ref.dtype
        )


def merge(near, near_stats, far, far_stats, out_weight, pieces):
    rows = near.shape[0]
    width = out_weight.shape[1]
    vmem = pl.BlockSpec(memory_space=pltpu.VMEM)
    return pl.pallas_call(
        merge_kernel,
        out_shape=jax.ShapeDtypeStruct((pieces, rows, width // pieces), jnp.bfloat16),
        in_specs=[vmem] * 5,
        out_specs=vmem,
        scratch_shapes=[pltpu.VMEM((rows, rows), jnp.float32)],
        cost_estimate=pl.CostEstimate(
            flops=2 * rows * near.shape[1] * width, transcendentals=0,
            bytes_accessed=out_weight.size * 2 + rows * width * 2,
        ),
    )(near, near_stats, far, far_stats, out_weight)


def shards(queries, keys, values, docs, out_weight):
    rows = queries.shape[0]
    head_dim = HEAD_DIM
    ctx = lax.psum(1, "ctx")
    tp = lax.psum(1, "tp")
    my_index = lax.axis_index("ctx")
    plane = my_index // PLANE
    slot = my_index % PLANE
    planes = ctx // PLANE

    shards_back = -(-(MAX_DOC - 1) // rows)
    reach = min(-(-(shards_back + PLANE - 1) // PLANE), planes - 1)
    hops = reach // 2
    far = hops + 1

    doc_rows = jnp.zeros((DOC_ROWS, 2 * head_dim), jnp.bfloat16)
    doc_rows = doc_rows.at[0, :rows].set(docs.astype(jnp.bfloat16))
    block = jnp.concatenate([jnp.concatenate([keys, values], axis=1), doc_rows], axis=0)

    query_docs = jnp.zeros((DOC_ROWS, queries.shape[1]), jnp.bfloat16)
    query_docs = query_docs.at[0, :rows].set(docs.astype(jnp.bfloat16))
    packed_queries = jnp.concatenate([queries, query_docs], axis=0)
    back = [(s, s - PLANE * far) for s in range(PLANE * far, ctx)]
    visiting = lax.ppermute(packed_queries, "ctx", back)

    plane_blocks = [block]
    for offset in range(1, PLANE):
        plane_blocks.append(lax.ppermute(block, "ctx", [(s, s ^ offset) for s in range(ctx)]))
    current = jnp.stack(plane_blocks)
    forward = [(s, s + PLANE) for s in range(ctx - PLANE)]
    collected = [current]
    for hop in range(hops):
        current = lax.ppermute(current, "ctx", forward)
        collected.append(current)
    blocks = collected

    hop_ids = jnp.arange(hops + 1, dtype=jnp.int32)[:, None, None]
    offsets = jnp.arange(PLANE, dtype=jnp.int32)[None, :, None]
    tokens = jnp.arange(rows, dtype=jnp.int32)[None, None, :]
    key_shard = PLANE * (plane - hop_ids) + (slot ^ offsets)
    key_pos = (key_shard * rows + tokens).reshape(1, -1)
    key_doc = jnp.concatenate(
        [b[:, rows, :rows].astype(jnp.int32).reshape(1, -1) for b in blocks], axis=1
    )

    offsets_in_shard = jnp.arange(rows, dtype=jnp.int32).reshape(rows, 1)
    visit_pos = (my_index + PLANE * far) * rows + offsets_in_shard
    visit_doc = visiting[rows, :rows].astype(jnp.int32).reshape(rows, 1)
    visit_out, visit_stats, visit_rows = partial(
        visiting, blocks, key_pos, key_doc, visit_pos, visit_doc, jnp.bfloat16
    )
    ahead = [(s, s + PLANE * far) for s in range(ctx - PLANE * far)]
    far_out = lax.ppermute(visit_out, "ctx", ahead)
    far_rows = lax.ppermute(visit_rows, "ctx", ahead)

    query_pos = my_index * rows + offsets_in_shard
    near_out, near_stats, _ = partial(
        queries, blocks, key_pos, key_doc, query_pos, docs.reshape(rows, 1), jnp.float32
    )
    has_far = plane >= far
    heads = near_stats.shape[1] // 2
    kind = jnp.arange(2 * heads, dtype=jnp.int32)[:, None]
    far_rows = jnp.where(has_far, far_rows, jnp.where(kind < heads, neg_large, 0.0))
    chunks = merge(near_out, near_stats, far_out, far_rows, out_weight, tp)

    received = lax.all_to_all(chunks, "tp", 0, 0, tiled=True)
    mixed = jnp.sum(received.astype(jnp.float32), axis=0)
    return mixed.astype(jnp.bfloat16)


def solution(mesh):
    placed = (P("ctx", "tp"), P("ctx", "tp"), P("ctx", "tp"), P("ctx"), P("tp", None))
    return jax.shard_map(
        shards, mesh=mesh, in_specs=placed, out_specs=P("ctx", "tp"), check_vma=False
    )
```

```python
import math

import jax
import jax.numpy as jnp
from jax import lax
from jax.experimental import pallas as pl
from jax.experimental.pallas import tpu as pltpu
from jax.sharding import PartitionSpec as P

HEAD_DIM = 128
MAX_DOC = 4224
PLANE = 4
DOC_ROWS = 8
neg_large = -1e30


def partial_kernel(*refs):
    query_ref = refs[0]
    block_refs = refs[1:-8]
    (key_pos_ref, key_doc_ref, query_pos_ref, query_doc_ref, out_ref, stats_ref,
     rows_ref, square_ref) = refs[-8:]
    rows = query_pos_ref.shape[0]
    width = query_ref.shape[1]
    head_dim = block_refs[0].shape[-1] // 2
    heads = width // head_dim
    key_part = jnp.concatenate(
        [ref[:, :rows, :head_dim].reshape(ref.shape[0] * rows, head_dim) for ref in block_refs],
        axis=0,
    )
    value_part = jnp.concatenate(
        [ref[:, :rows, head_dim:].reshape(ref.shape[0] * rows, head_dim) for ref in block_refs],
        axis=0,
    )
    allowed = (
        (key_pos_ref[...] <= query_pos_ref[...])
        & (key_pos_ref[...] >= 0)
        & (key_doc_ref[...] == query_doc_ref[...])
    )
    bias = jnp.where(allowed, 0.0, neg_large)
    seen = jnp.max(jnp.where(allowed, 1.0, 0.0), axis=1, keepdims=True) > 0.0
    scale = 1.0 / math.sqrt(head_dim)
    for head in range(heads):
        query = query_ref[:rows, head * head_dim:(head + 1) * head_dim]
        scores = lax.dot_general(
            query, key_part, (((1,), (1,)), ((), ())), preferred_element_type=jnp.float32
        )
        scores = scores * scale + bias
        peak = jnp.max(scores, axis=1, keepdims=True)
        weight = jnp.exp(scores - peak)
        total = jnp.where(seen, jnp.sum(weight, axis=1, keepdims=True), 0.0)
        summed = jnp.dot(
            weight.astype(jnp.bfloat16), value_part, preferred_element_type=jnp.float32
        )
        normed = jnp.where(seen, summed / jnp.maximum(total, 1e-30), 0.0)
        out_ref[:, head * head_dim:(head + 1) * head_dim] = normed.astype(out_ref.dtype)
        stats_ref[:, head:head + 1] = jnp.where(seen, peak, neg_large)
        stats_ref[:, heads + head:heads + head + 1] = total
    square_ref[...] = jnp.zeros_like(square_ref)
    square_ref[:, :2 * heads] = stats_ref[...]
    rows_ref[...] = jnp.transpose(square_ref[...])[:2 * heads]


def partial(query, blocks, key_pos, key_doc, query_pos, query_doc, out_dtype):
    rows = query_pos.shape[0]
    width = query.shape[1]
    heads = width // HEAD_DIM
    tokens = key_pos.shape[1]
    vmem = pl.BlockSpec(memory_space=pltpu.VMEM)
    return pl.pallas_call(
        partial_kernel,
        out_shape=(
            jax.ShapeDtypeStruct((rows, width), out_dtype),
            jax.ShapeDtypeStruct((rows, 2 * heads), jnp.float32),
            jax.ShapeDtypeStruct((2 * heads, rows), jnp.float32),
        ),
        in_specs=[vmem] * (5 + len(blocks)),
        out_specs=(vmem, vmem, vmem),
        scratch_shapes=[pltpu.VMEM((rows, rows), jnp.float32)],
        cost_estimate=pl.CostEstimate(
            flops=4 * rows * tokens * width, transcendentals=rows * tokens * heads,
            bytes_accessed=sum(b.size for b in blocks) * 2 + query.size * 2 + rows * width * 4,
        ),
    )(query, *blocks, key_pos, key_doc, query_pos, query_doc)


def merge_kernel(near_ref, near_stats_ref, far_ref, far_rows_ref, weight_ref, out_ref,
                 square_ref):
    rows, width = near_ref.shape
    heads = near_stats_ref.shape[1] // 2
    head_dim = width // heads
    square_ref[...] = jnp.zeros_like(square_ref)
    square_ref[:2 * heads, :] = far_rows_ref[...]
    far_stats = jnp.transpose(square_ref[...])
    outputs = []
    for head in range(heads):
        near_peak = near_stats_ref[:, head:head + 1]
        near_total = near_stats_ref[:, heads + head:heads + head + 1]
        far_peak = far_stats[:, head:head + 1]
        far_total = far_stats[:, heads + head:heads + head + 1]
        peak = jnp.maximum(near_peak, far_peak)
        near_share = near_total * jnp.exp(near_peak - peak)
        far_share = far_total * jnp.exp(far_peak - peak)
        columns = slice(head * head_dim, (head + 1) * head_dim)
        summed = (
            near_ref[:, columns].astype(jnp.float32) * near_share
            + far_ref[:, columns].astype(jnp.float32) * far_share
        )
        outputs.append((summed / (near_share + far_share)).astype(jnp.bfloat16))
    attention = jnp.concatenate(outputs, axis=1)
    partial_terms = jnp.dot(attention, weight_ref[...], preferred_element_type=jnp.float32)
    pieces, _, piece_width = out_ref.shape
    for piece in range(pieces):
        out_ref[piece] = partial_terms[:, piece * piece_width:(piece + 1) * piece_width].astype(
            out_ref.dtype
        )


def merge(near, near_stats, far, far_stats, out_weight, pieces):
    rows = near.shape[0]
    width = out_weight.shape[1]
    vmem = pl.BlockSpec(memory_space=pltpu.VMEM)
    return pl.pallas_call(
        merge_kernel,
        out_shape=jax.ShapeDtypeStruct((pieces, rows, width // pieces), jnp.bfloat16),
        in_specs=[vmem] * 5,
        out_specs=vmem,
        scratch_shapes=[pltpu.VMEM((rows, rows), jnp.float32)],
        cost_estimate=pl.CostEstimate(
            flops=2 * rows * near.shape[1] * width, transcendentals=0,
            bytes_accessed=out_weight.size * 2 + rows * width * 2,
        ),
    )(near, near_stats, far, far_stats, out_weight)


def shards(queries, keys, values, docs, out_weight):
    rows = queries.shape[0]
    head_dim = HEAD_DIM
    ctx = lax.psum(1, "ctx")
    tp = lax.psum(1, "tp")
    my_index = lax.axis_index("ctx")
    plane = my_index // PLANE
    slot = my_index % PLANE
    planes = ctx // PLANE

    shards_back = -(-(MAX_DOC - 1) // rows)
    reach = min(-(-(shards_back + PLANE - 1) // PLANE), planes - 1)
    hops = reach // 2
    far = hops + 1

    doc_rows = jnp.zeros((DOC_ROWS, 2 * head_dim), jnp.bfloat16)
    doc_rows = doc_rows.at[0, :rows].set(docs.astype(jnp.bfloat16))
    block = jnp.concatenate([jnp.concatenate([keys, values], axis=1), doc_rows], axis=0)

    query_docs = jnp.zeros((DOC_ROWS, queries.shape[1]), jnp.bfloat16)
    query_docs = query_docs.at[0, :rows].set(docs.astype(jnp.bfloat16))
    packed_queries = jnp.concatenate([queries, query_docs], axis=0)
    back = [(s, s - PLANE * far) for s in range(PLANE * far, ctx)]
    visiting = lax.ppermute(packed_queries, "ctx", back)

    plane_blocks = [block]
    for offset in range(1, PLANE):
        plane_blocks.append(lax.ppermute(block, "ctx", [(s, s ^ offset) for s in range(ctx)]))
    current = jnp.stack(plane_blocks)
    forward = [(s, s + PLANE) for s in range(ctx - PLANE)]
    collected = [current]
    for hop in range(hops):
        current = lax.ppermute(current, "ctx", forward)
        collected.append(current)
    blocks = collected

    hop_ids = jnp.arange(hops + 1, dtype=jnp.int32)[:, None, None]
    offsets = jnp.arange(PLANE, dtype=jnp.int32)[None, :, None]
    tokens = jnp.arange(rows, dtype=jnp.int32)[None, None, :]
    key_shard = PLANE * (plane - hop_ids) + (slot ^ offsets)
    key_pos = (key_shard * rows + tokens).reshape(1, -1)
    key_doc = jnp.concatenate(
        [b[:, rows, :rows].astype(jnp.int32).reshape(1, -1) for b in blocks], axis=1
    )

    last = PLANE - 1
    oldest = lax.dynamic_index_in_dim(collected[hops], slot ^ last, 0, keepdims=True)
    far_blocks = collected[:hops] + [oldest]
    far_count = hops * PLANE * rows
    oldest_pos = (PLANE * (plane - hops) + last) * rows + jnp.arange(rows, dtype=jnp.int32)
    far_key_pos = jnp.concatenate([key_pos[:, :far_count], oldest_pos[None]], axis=1)
    far_key_doc = jnp.concatenate(
        [key_doc[:, :far_count], oldest[0, rows, :rows].astype(jnp.int32)[None]], axis=1
    )

    offsets_in_shard = jnp.arange(rows, dtype=jnp.int32).reshape(rows, 1)
    visit_pos = (my_index + PLANE * far) * rows + offsets_in_shard
    visit_doc = visiting[rows, :rows].astype(jnp.int32).reshape(rows, 1)
    visit_out, visit_stats, visit_rows = partial(
        visiting, far_blocks, far_key_pos, far_key_doc, visit_pos, visit_doc, jnp.bfloat16
    )
    ahead = [(s, s + PLANE * far) for s in range(ctx - PLANE * far)]
    far_out = lax.ppermute(visit_out, "ctx", ahead)
    far_rows = lax.ppermute(visit_rows, "ctx", ahead)

    query_pos = my_index * rows + offsets_in_shard
    near_out, near_stats, _ = partial(
        queries, blocks, key_pos, key_doc, query_pos, docs.reshape(rows, 1), jnp.float32
    )
    has_far = plane >= far
    heads = near_stats.shape[1] // 2
    kind = jnp.arange(2 * heads, dtype=jnp.int32)[:, None]
    far_rows = jnp.where(has_far, far_rows, jnp.where(kind < heads, neg_large, 0.0))
    chunks = merge(near_out, near_stats, far_out, far_rows, out_weight, tp)

    received = lax.all_to_all(chunks, "tp", 0, 0, tiled=True)
    mixed = jnp.sum(received.astype(jnp.float32), axis=0)
    return mixed.astype(jnp.bfloat16)


def solution(mesh):
    placed = (P("ctx", "tp"), P("ctx", "tp"), P("ctx", "tp"), P("ctx"), P("tp", None))
    return jax.shard_map(
        shards, mesh=mesh, in_specs=placed, out_specs=P("ctx", "tp"), check_vma=False
    )
```

```python
import math

import jax
import jax.numpy as jnp
from jax import lax
from jax.experimental import pallas as pl
from jax.experimental.pallas import tpu as pltpu
from jax.sharding import PartitionSpec as P

HEAD_DIM = 128
MAX_DOC = 4224
PLANE = 4
DOC_ROWS = 8
neg_large = -1e30


def partial_kernel(*refs):
    query_ref = refs[0]
    block_refs = refs[1:-7]
    (key_pos_ref, query_pos_ref, query_doc_ref, out_ref, stats_ref,
     rows_ref, square_ref) = refs[-7:]
    rows = query_pos_ref.shape[0]
    width = query_ref.shape[1]
    head_dim = block_refs[0].shape[-1] // 2
    heads = width // head_dim
    key_part = jnp.concatenate(
        [ref[:, :rows, :head_dim].reshape(ref.shape[0] * rows, head_dim) for ref in block_refs],
        axis=0,
    )
    value_part = jnp.concatenate(
        [ref[:, :rows, head_dim:].reshape(ref.shape[0] * rows, head_dim) for ref in block_refs],
        axis=0,
    )
    key_doc = jnp.concatenate(
        [ref[shard, rows:rows + 1, :rows].astype(jnp.float32)
         for ref in block_refs for shard in range(ref.shape[0])],
        axis=1,
    )
    allowed = (
        (key_pos_ref[...] <= query_pos_ref[...])
        & (key_pos_ref[...] >= 0)
        & (key_doc == query_doc_ref[...].astype(jnp.float32))
    )
    bias = jnp.where(allowed, 0.0, neg_large)
    seen = jnp.max(jnp.where(allowed, 1.0, 0.0), axis=1, keepdims=True) > 0.0
    scale = 1.0 / math.sqrt(head_dim)
    for head in range(heads):
        query = query_ref[:rows, head * head_dim:(head + 1) * head_dim]
        scores = lax.dot_general(
            query, key_part, (((1,), (1,)), ((), ())), preferred_element_type=jnp.float32
        )
        scores = scores * scale + bias
        peak = jnp.max(scores, axis=1, keepdims=True)
        weight = jnp.exp(scores - peak)
        total = jnp.where(seen, jnp.sum(weight, axis=1, keepdims=True), 0.0)
        summed = jnp.dot(
            weight.astype(jnp.bfloat16), value_part, preferred_element_type=jnp.float32
        )
        normed = jnp.where(seen, summed / jnp.maximum(total, 1e-30), 0.0)
        out_ref[:, head * head_dim:(head + 1) * head_dim] = normed.astype(out_ref.dtype)
        stats_ref[:, head:head + 1] = jnp.where(seen, peak, neg_large)
        stats_ref[:, heads + head:heads + head + 1] = total
    square_ref[...] = jnp.zeros_like(square_ref)
    square_ref[:, :2 * heads] = stats_ref[...]
    rows_ref[...] = jnp.transpose(square_ref[...])[:2 * heads]


def partial(query, blocks, key_pos, query_pos, query_doc, out_dtype):
    rows = query_pos.shape[0]
    width = query.shape[1]
    heads = width // HEAD_DIM
    tokens = key_pos.shape[1]
    vmem = pl.BlockSpec(memory_space=pltpu.VMEM)
    return pl.pallas_call(
        partial_kernel,
        out_shape=(
            jax.ShapeDtypeStruct((rows, width), out_dtype),
            jax.ShapeDtypeStruct((rows, 2 * heads), jnp.float32),
            jax.ShapeDtypeStruct((2 * heads, rows), jnp.float32),
        ),
        in_specs=[vmem] * (4 + len(blocks)),
        out_specs=(vmem, vmem, vmem),
        scratch_shapes=[pltpu.VMEM((rows, rows), jnp.float32)],
        cost_estimate=pl.CostEstimate(
            flops=4 * rows * tokens * width, transcendentals=rows * tokens * heads,
            bytes_accessed=sum(b.size for b in blocks) * 2 + query.size * 2 + rows * width * 4,
        ),
    )(query, *blocks, key_pos, query_pos, query_doc)


def merge_kernel(near_ref, near_stats_ref, far_ref, far_rows_ref, weight_ref, out_ref,
                 square_ref):
    rows, width = near_ref.shape
    heads = near_stats_ref.shape[1] // 2
    head_dim = width // heads
    square_ref[...] = jnp.zeros_like(square_ref)
    square_ref[:2 * heads, :] = far_rows_ref[...]
    far_stats = jnp.transpose(square_ref[...])
    outputs = []
    for head in range(heads):
        near_peak = near_stats_ref[:, head:head + 1]
        near_total = near_stats_ref[:, heads + head:heads + head + 1]
        far_peak = far_stats[:, head:head + 1]
        far_total = far_stats[:, heads + head:heads + head + 1]
        peak = jnp.maximum(near_peak, far_peak)
        near_share = near_total * jnp.exp(near_peak - peak)
        far_share = far_total * jnp.exp(far_peak - peak)
        columns = slice(head * head_dim, (head + 1) * head_dim)
        summed = (
            near_ref[:, columns].astype(jnp.float32) * near_share
            + far_ref[:, columns].astype(jnp.float32) * far_share
        )
        outputs.append((summed / (near_share + far_share)).astype(jnp.bfloat16))
    attention = jnp.concatenate(outputs, axis=1)
    partial_terms = jnp.dot(attention, weight_ref[...], preferred_element_type=jnp.float32)
    pieces, _, piece_width = out_ref.shape
    for piece in range(pieces):
        out_ref[piece] = partial_terms[:, piece * piece_width:(piece + 1) * piece_width].astype(
            out_ref.dtype
        )


def merge(near, near_stats, far, far_stats, out_weight, pieces):
    rows = near.shape[0]
    width = out_weight.shape[1]
    vmem = pl.BlockSpec(memory_space=pltpu.VMEM)
    return pl.pallas_call(
        merge_kernel,
        out_shape=jax.ShapeDtypeStruct((pieces, rows, width // pieces), jnp.bfloat16),
        in_specs=[vmem] * 5,
        out_specs=vmem,
        scratch_shapes=[pltpu.VMEM((rows, rows), jnp.float32)],
        cost_estimate=pl.CostEstimate(
            flops=2 * rows * near.shape[1] * width, transcendentals=0,
            bytes_accessed=out_weight.size * 2 + rows * width * 2,
        ),
    )(near, near_stats, far, far_stats, out_weight)


def shards(queries, keys, values, docs, out_weight):
    rows = queries.shape[0]
    head_dim = HEAD_DIM
    ctx = lax.psum(1, "ctx")
    tp = lax.psum(1, "tp")
    my_index = lax.axis_index("ctx")
    plane = my_index // PLANE
    slot = my_index % PLANE
    planes = ctx // PLANE

    shards_back = -(-(MAX_DOC - 1) // rows)
    reach = min(-(-(shards_back + PLANE - 1) // PLANE), planes - 1)
    hops = reach // 2
    far = hops + 1

    doc_rows = jnp.zeros((DOC_ROWS, 2 * head_dim), jnp.bfloat16)
    doc_rows = doc_rows.at[0, :rows].set(docs.astype(jnp.bfloat16))
    block = jnp.concatenate([jnp.concatenate([keys, values], axis=1), doc_rows], axis=0)

    query_docs = jnp.zeros((DOC_ROWS, queries.shape[1]), jnp.bfloat16)
    query_docs = query_docs.at[0, :rows].set(docs.astype(jnp.bfloat16))
    packed_queries = jnp.concatenate([queries, query_docs], axis=0)
    back = [(s, s - PLANE * far) for s in range(PLANE * far, ctx)]
    visiting = lax.ppermute(packed_queries, "ctx", back)

    plane_blocks = [block]
    for offset in range(1, PLANE):
        plane_blocks.append(lax.ppermute(block, "ctx", [(s, s ^ offset) for s in range(ctx)]))
    current = jnp.stack(plane_blocks)
    forward = [(s, s + PLANE) for s in range(ctx - PLANE)]
    collected = [current]
    for hop in range(hops):
        current = lax.ppermute(current, "ctx", forward)
        collected.append(current)
    blocks = collected

    hop_ids = jnp.arange(hops + 1, dtype=jnp.int32)[:, None, None]
    offsets = jnp.arange(PLANE, dtype=jnp.int32)[None, :, None]
    tokens = jnp.arange(rows, dtype=jnp.int32)[None, None, :]
    key_shard = PLANE * (plane - hop_ids) + (slot ^ offsets)
    key_pos = (key_shard * rows + tokens).reshape(1, -1)

    offsets_in_shard = jnp.arange(rows, dtype=jnp.int32).reshape(rows, 1)
    visit_pos = (my_index + PLANE * far) * rows + offsets_in_shard
    visit_doc = visiting[rows, :rows].astype(jnp.int32).reshape(rows, 1)
    visit_out, visit_stats, visit_rows = partial(
        visiting, blocks, key_pos, visit_pos, visit_doc, jnp.bfloat16
    )
    ahead = [(s, s + PLANE * far) for s in range(ctx - PLANE * far)]
    far_out = lax.ppermute(visit_out, "ctx", ahead)
    far_rows = lax.ppermute(visit_rows, "ctx", ahead)

    query_pos = my_index * rows + offsets_in_shard
    near_out, near_stats, _ = partial(
        queries, blocks, key_pos, query_pos, docs.reshape(rows, 1), jnp.float32
    )
    has_far = plane >= far
    heads = near_stats.shape[1] // 2
    kind = jnp.arange(2 * heads, dtype=jnp.int32)[:, None]
    far_rows = jnp.where(has_far, far_rows, jnp.where(kind < heads, neg_large, 0.0))
    chunks = merge(near_out, near_stats, far_out, far_rows, out_weight, tp)

    received = lax.all_to_all(chunks, "tp", 0, 0, tiled=True)
    mixed = jnp.sum(received.astype(jnp.float32), axis=0)
    return mixed.astype(jnp.bfloat16)


def solution(mesh):
    placed = (P("ctx", "tp"), P("ctx", "tp"), P("ctx", "tp"), P("ctx"), P("tp", None))
    return jax.shard_map(
        shards, mesh=mesh, in_specs=placed, out_specs=P("ctx", "tp"), check_vma=False
    )
```

```python
import math

import jax
import jax.numpy as jnp
from jax import lax
from jax.experimental import pallas as pl
from jax.experimental.pallas import tpu as pltpu
from jax.sharding import PartitionSpec as P

HEAD_DIM = 128
MAX_DOC = 4224
PLANE = 4
DOC_ROWS = 8
neg_large = -1e30


def partial_kernel(*refs):
    query_ref = refs[0]
    block_refs = refs[1:-8]
    (key_pos_ref, key_doc_ref, query_pos_ref, query_doc_ref, out_ref, stats_ref,
     rows_ref, square_ref) = refs[-8:]
    rows = query_pos_ref.shape[0]
    width = query_ref.shape[1]
    head_dim = block_refs[0].shape[-1] // 2
    heads = width // head_dim
    key_part = jnp.concatenate(
        [ref[:, :rows, :head_dim].reshape(ref.shape[0] * rows, head_dim) for ref in block_refs],
        axis=0,
    )
    value_part = jnp.concatenate(
        [ref[:, :rows, head_dim:].reshape(ref.shape[0] * rows, head_dim) for ref in block_refs],
        axis=0,
    )
    allowed = (
        (key_pos_ref[...] <= query_pos_ref[...])
        & (key_pos_ref[...] >= 0)
        & (key_doc_ref[...] == query_doc_ref[...])
    )
    bias = jnp.where(allowed, 0.0, neg_large)
    seen = jnp.max(jnp.where(allowed, 1.0, 0.0), axis=1, keepdims=True) > 0.0
    scale = 1.0 / math.sqrt(head_dim)
    for head in range(heads):
        query = query_ref[:rows, head * head_dim:(head + 1) * head_dim]
        scores = lax.dot_general(
            query, key_part, (((1,), (1,)), ((), ())), preferred_element_type=jnp.float32
        )
        scores = scores * scale + bias
        peak = jnp.max(scores, axis=1, keepdims=True)
        weight = jnp.exp(scores - peak)
        total = jnp.where(seen, jnp.sum(weight, axis=1, keepdims=True), 0.0)
        summed = jnp.dot(
            weight.astype(jnp.bfloat16), value_part, preferred_element_type=jnp.float32
        )
        normed = jnp.where(seen, summed / jnp.maximum(total, 1e-30), 0.0)
        out_ref[:, head * head_dim:(head + 1) * head_dim] = normed.astype(out_ref.dtype)
        stats_ref[:, head:head + 1] = jnp.where(seen, peak, neg_large)
        stats_ref[:, heads + head:heads + head + 1] = total
    square_ref[...] = jnp.zeros_like(square_ref)
    square_ref[:, :2 * heads] = stats_ref[...]
    rows_ref[...] = jnp.transpose(square_ref[...])[:2 * heads]


def partial(query, blocks, key_pos, key_doc, query_pos, query_doc, out_dtype):
    rows = query_pos.shape[0]
    width = query.shape[1]
    heads = width // HEAD_DIM
    tokens = key_pos.shape[1]
    vmem = pl.BlockSpec(memory_space=pltpu.VMEM)
    return pl.pallas_call(
        partial_kernel,
        out_shape=(
            jax.ShapeDtypeStruct((rows, width), out_dtype),
            jax.ShapeDtypeStruct((rows, 2 * heads), jnp.float32),
            jax.ShapeDtypeStruct((2 * heads, rows), jnp.float32),
        ),
        in_specs=[vmem] * (5 + len(blocks)),
        out_specs=(vmem, vmem, vmem),
        scratch_shapes=[pltpu.VMEM((rows, rows), jnp.float32)],
        cost_estimate=pl.CostEstimate(
            flops=4 * rows * tokens * width, transcendentals=rows * tokens * heads,
            bytes_accessed=sum(b.size for b in blocks) * 2 + query.size * 2 + rows * width * 4,
        ),
    )(query, *blocks, key_pos, key_doc, query_pos, query_doc)


def merge_kernel(near_ref, near_stats_ref, far_ref, far_rows_ref, weight_ref, out_ref,
                 square_ref):
    rows, width = near_ref.shape
    heads = near_stats_ref.shape[1] // 2
    head_dim = width // heads
    square_ref[...] = jnp.zeros_like(square_ref)
    square_ref[:2 * heads, :] = far_rows_ref[...]
    far_stats = jnp.transpose(square_ref[...])
    outputs = []
    for head in range(heads):
        near_peak = near_stats_ref[:, head:head + 1]
        near_total = near_stats_ref[:, heads + head:heads + head + 1]
        far_peak = far_stats[:, head:head + 1]
        far_total = far_stats[:, heads + head:heads + head + 1]
        peak = jnp.maximum(near_peak, far_peak)
        near_share = near_total * jnp.exp(near_peak - peak)
        far_share = far_total * jnp.exp(far_peak - peak)
        columns = slice(head * head_dim, (head + 1) * head_dim)
        summed = (
            near_ref[:, columns].astype(jnp.float32) * near_share
            + far_ref[:, columns].astype(jnp.float32) * far_share
        )
        outputs.append((summed / (near_share + far_share)).astype(jnp.bfloat16))
    attention = jnp.concatenate(outputs, axis=1)
    partial_terms = jnp.dot(attention, weight_ref[...], preferred_element_type=jnp.float32)
    pieces, _, piece_width = out_ref.shape
    for piece in range(pieces):
        out_ref[piece] = partial_terms[:, piece * piece_width:(piece + 1) * piece_width].astype(
            out_ref.dtype
        )


def merge(near, near_stats, far, far_stats, out_weight, pieces):
    rows = near.shape[0]
    width = out_weight.shape[1]
    vmem = pl.BlockSpec(memory_space=pltpu.VMEM)
    return pl.pallas_call(
        merge_kernel,
        out_shape=jax.ShapeDtypeStruct((pieces, rows, width // pieces), jnp.bfloat16),
        in_specs=[vmem] * 5,
        out_specs=vmem,
        scratch_shapes=[pltpu.VMEM((rows, rows), jnp.float32)],
        cost_estimate=pl.CostEstimate(
            flops=2 * rows * near.shape[1] * width, transcendentals=0,
            bytes_accessed=out_weight.size * 2 + rows * width * 2,
        ),
    )(near, near_stats, far, far_stats, out_weight)


def shards(queries, keys, values, docs, out_weight):
    rows = queries.shape[0]
    head_dim = HEAD_DIM
    ctx = lax.psum(1, "ctx")
    tp = lax.psum(1, "tp")
    my_index = lax.axis_index("ctx")
    plane = my_index // PLANE
    slot = my_index % PLANE
    planes = ctx // PLANE

    shards_back = -(-(MAX_DOC - 1) // rows)
    reach = min(-(-(shards_back + PLANE - 1) // PLANE), planes - 1)
    hops = reach // 2
    far = hops + 1

    doc_rows = jnp.zeros((DOC_ROWS, 2 * head_dim), jnp.bfloat16)
    doc_rows = doc_rows.at[0, :rows].set(docs.astype(jnp.bfloat16))
    block = jnp.concatenate([jnp.concatenate([keys, values], axis=1), doc_rows], axis=0)

    query_docs = jnp.zeros((DOC_ROWS, queries.shape[1]), jnp.bfloat16)
    query_docs = query_docs.at[0, :rows].set(docs.astype(jnp.bfloat16))
    packed_queries = jnp.concatenate([queries, query_docs], axis=0)
    back = [(s, s - PLANE * far) for s in range(PLANE * far, ctx)]
    visiting = lax.ppermute(packed_queries, "ctx", back)

    plane_blocks = [block]
    for offset in range(1, PLANE):
        plane_blocks.append(lax.ppermute(block, "ctx", [(s, s ^ offset) for s in range(ctx)]))
    current = jnp.stack(plane_blocks)
    forward = [(s, s + PLANE) for s in range(ctx - PLANE)]
    collected = [current]
    for hop in range(hops):
        current = lax.ppermute(current, "ctx", forward)
        collected.append(current)
    blocks = collected

    hop_ids = jnp.arange(hops + 1, dtype=jnp.int32)[:, None, None]
    offsets = jnp.arange(PLANE, dtype=jnp.int32)[None, :, None]
    tokens = jnp.arange(rows, dtype=jnp.int32)[None, None, :]
    key_shard = PLANE * (plane - hop_ids) + (slot ^ offsets)
    key_pos = (key_shard * rows + tokens).reshape(1, -1)
    key_doc = jnp.concatenate(
        [b[:, rows, :rows].astype(jnp.int32).reshape(1, -1) for b in blocks], axis=1
    )

    offsets_in_shard = jnp.arange(rows, dtype=jnp.int32).reshape(rows, 1)
    visit_pos = (my_index + PLANE * far) * rows + offsets_in_shard
    visit_doc = visiting[rows, :rows].astype(jnp.int32).reshape(rows, 1)
    visit_out, visit_stats, visit_rows = partial(
        visiting, blocks, key_pos, key_doc, visit_pos, visit_doc, jnp.bfloat16
    )
    ahead = [(s, s + PLANE * far) for s in range(ctx - PLANE * far)]
    far_out = lax.ppermute(visit_out, "ctx", ahead)
    far_rows = lax.ppermute(visit_rows, "ctx", ahead)

    query_pos = my_index * rows + offsets_in_shard
    near_out, near_stats, _ = partial(
        queries, blocks, key_pos, key_doc, query_pos, docs.reshape(rows, 1), jnp.bfloat16
    )
    has_far = plane >= far
    heads = near_stats.shape[1] // 2
    kind = jnp.arange(2 * heads, dtype=jnp.int32)[:, None]
    far_rows = jnp.where(has_far, far_rows, jnp.where(kind < heads, neg_large, 0.0))
    chunks = merge(near_out, near_stats, far_out, far_rows, out_weight, tp)

    received = lax.all_to_all(chunks, "tp", 0, 0, tiled=True)
    mixed = jnp.sum(received.astype(jnp.float32), axis=0)
    return mixed.astype(jnp.bfloat16)


def solution(mesh):
    placed = (P("ctx", "tp"), P("ctx", "tp"), P("ctx", "tp"), P("ctx"), P("tp", None))
    return jax.shard_map(
        shards, mesh=mesh, in_specs=placed, out_specs=P("ctx", "tp"), check_vma=False
    )
```

```python
import math

import jax
import jax.numpy as jnp
from jax import lax
from jax.experimental import pallas as pl
from jax.experimental.pallas import tpu as pltpu
from jax.sharding import PartitionSpec as P

HEAD_DIM = 128
MAX_DOC = 4224
PLANE = 4
DOC_ROWS = 8
neg_large = -1e30


def partial_kernel(*refs):
    query_ref = refs[0]
    block_refs = refs[1:-8]
    (key_pos_ref, key_doc_ref, query_pos_ref, query_doc_ref, out_ref, stats_ref,
     rows_ref, square_ref) = refs[-8:]
    rows = query_pos_ref.shape[0]
    width = query_ref.shape[1]
    head_dim = block_refs[0].shape[-1] // 2
    heads = width // head_dim
    key_part = jnp.concatenate(
        [ref[:, :rows, :head_dim].reshape(ref.shape[0] * rows, head_dim) for ref in block_refs],
        axis=0,
    )
    value_part = jnp.concatenate(
        [ref[:, :rows, head_dim:].reshape(ref.shape[0] * rows, head_dim) for ref in block_refs],
        axis=0,
    )
    allowed = (
        (key_pos_ref[...] <= query_pos_ref[...])
        & (key_pos_ref[...] >= 0)
        & (key_doc_ref[...] == query_doc_ref[...])
    )
    bias = jnp.where(allowed, 0.0, neg_large)
    seen = jnp.max(jnp.where(allowed, 1.0, 0.0), axis=1, keepdims=True) > 0.0
    scale = 1.0 / math.sqrt(head_dim)
    for head in range(heads):
        query = query_ref[:rows, head * head_dim:(head + 1) * head_dim]
        scores = lax.dot_general(
            query, key_part, (((1,), (1,)), ((), ())), preferred_element_type=jnp.float32
        )
        scores = scores * scale + bias
        peak = jnp.max(scores, axis=1, keepdims=True)
        weight = jnp.exp(scores - peak)
        total = jnp.where(seen, jnp.sum(weight, axis=1, keepdims=True), 0.0)
        summed = jnp.dot(
            weight.astype(jnp.bfloat16), value_part, preferred_element_type=jnp.float32
        )
        normed = jnp.where(seen, summed / jnp.maximum(total, 1e-30), 0.0)
        out_ref[:, head * head_dim:(head + 1) * head_dim] = normed.astype(out_ref.dtype)
        stats_ref[:, head:head + 1] = jnp.where(seen, peak, neg_large)
        stats_ref[:, heads + head:heads + head + 1] = total
    square_ref[...] = jnp.zeros_like(square_ref)
    square_ref[:, :2 * heads] = stats_ref[...]
    rows_ref[...] = jnp.transpose(square_ref[...])[:2 * heads]


def partial(query, blocks, key_pos, key_doc, query_pos, query_doc, out_dtype):
    rows = query_pos.shape[0]
    width = query.shape[1]
    heads = width // HEAD_DIM
    tokens = key_pos.shape[1]
    vmem = pl.BlockSpec(memory_space=pltpu.VMEM)
    return pl.pallas_call(
        partial_kernel,
        out_shape=(
            jax.ShapeDtypeStruct((rows, width), out_dtype),
            jax.ShapeDtypeStruct((rows, 2 * heads), jnp.float32),
            jax.ShapeDtypeStruct((2 * heads, rows), jnp.float32),
        ),
        in_specs=[vmem] * (5 + len(blocks)),
        out_specs=(vmem, vmem, vmem),
        scratch_shapes=[pltpu.VMEM((rows, rows), jnp.float32)],
        cost_estimate=pl.CostEstimate(
            flops=4 * rows * tokens * width, transcendentals=rows * tokens * heads,
            bytes_accessed=sum(b.size for b in blocks) * 2 + query.size * 2 + rows * width * 4,
        ),
    )(query, *blocks, key_pos, key_doc, query_pos, query_doc)


def merge_kernel(near_ref, near_stats_ref, far_ref, far_rows_ref, weight_ref, out_ref,
                 square_ref):
    rows, width = near_ref.shape
    heads = near_stats_ref.shape[1] // 2
    head_dim = width // heads
    square_ref[...] = jnp.zeros_like(square_ref)
    square_ref[:2 * heads, :] = far_rows_ref[...]
    far_stats = jnp.transpose(square_ref[...])
    outputs = []
    for head in range(heads):
        near_peak = near_stats_ref[:, head:head + 1]
        near_total = near_stats_ref[:, heads + head:heads + head + 1]
        far_peak = far_stats[:, head:head + 1]
        far_total = far_stats[:, heads + head:heads + head + 1]
        peak = jnp.maximum(near_peak, far_peak)
        near_share = near_total * jnp.exp(near_peak - peak)
        far_share = far_total * jnp.exp(far_peak - peak)
        columns = slice(head * head_dim, (head + 1) * head_dim)
        summed = (
            near_ref[:, columns].astype(jnp.float32) * near_share
            + far_ref[:, columns].astype(jnp.float32) * far_share
        )
        outputs.append((summed / (near_share + far_share)).astype(jnp.bfloat16))
    attention = jnp.concatenate(outputs, axis=1)
    partial_terms = jnp.dot(attention, weight_ref[...], preferred_element_type=jnp.float32)
    pieces, _, piece_width = out_ref.shape
    for piece in range(pieces):
        out_ref[piece] = partial_terms[:, piece * piece_width:(piece + 1) * piece_width].astype(
            out_ref.dtype
        )


def merge(near, near_stats, far, far_stats, out_weight, pieces):
    rows = near.shape[0]
    width = out_weight.shape[1]
    vmem = pl.BlockSpec(memory_space=pltpu.VMEM)
    return pl.pallas_call(
        merge_kernel,
        out_shape=jax.ShapeDtypeStruct((pieces, rows, width // pieces), jnp.bfloat16),
        in_specs=[vmem] * 5,
        out_specs=vmem,
        scratch_shapes=[pltpu.VMEM((rows, rows), jnp.float32)],
        cost_estimate=pl.CostEstimate(
            flops=2 * rows * near.shape[1] * width, transcendentals=0,
            bytes_accessed=out_weight.size * 2 + rows * width * 2,
        ),
    )(near, near_stats, far, far_stats, out_weight)


def shards(queries, keys, values, docs, out_weight):
    rows = queries.shape[0]
    head_dim = HEAD_DIM
    ctx = lax.psum(1, "ctx")
    tp = lax.psum(1, "tp")
    my_index = lax.axis_index("ctx")
    plane = my_index // PLANE
    slot = my_index % PLANE
    planes = ctx // PLANE

    shards_back = -(-(MAX_DOC - 1) // rows)
    reach = min(-(-(shards_back + PLANE - 1) // PLANE), planes - 1)
    hops = reach // 2
    far = hops + 1

    doc_rows = jnp.zeros((DOC_ROWS, 2 * head_dim), jnp.bfloat16)
    doc_rows = doc_rows.at[0, :rows].set(docs.astype(jnp.bfloat16))
    block = jnp.concatenate([jnp.concatenate([keys, values], axis=1), doc_rows], axis=0)

    query_docs = jnp.zeros((DOC_ROWS, queries.shape[1]), jnp.bfloat16)
    query_docs = query_docs.at[0, :rows].set(docs.astype(jnp.bfloat16))
    packed_queries = jnp.concatenate([queries, query_docs], axis=0)
    back = [(s, s - PLANE * far) for s in range(PLANE * far, ctx)]
    visiting = lax.ppermute(packed_queries, "ctx", back)

    plane_blocks = [block]
    for offset in range(1, PLANE):
        plane_blocks.append(lax.ppermute(block, "ctx", [(s, s ^ offset) for s in range(ctx)]))
    current = jnp.stack(plane_blocks)
    forward = [(s, s + PLANE) for s in range(ctx - PLANE)]
    collected = [current]
    for hop in range(hops):
        current = lax.ppermute(current, "ctx", forward)
        collected.append(current)
    blocks = collected

    hop_ids = jnp.arange(hops + 1, dtype=jnp.int32)[:, None, None]
    offsets = jnp.arange(PLANE, dtype=jnp.int32)[None, :, None]
    tokens = jnp.arange(rows, dtype=jnp.int32)[None, None, :]
    key_shard = PLANE * (plane - hop_ids) + (slot ^ offsets)
    key_pos = (key_shard * rows + tokens).reshape(1, -1)
    key_doc = jnp.concatenate(
        [b[:, rows, :rows].astype(jnp.int32).reshape(1, -1) for b in blocks], axis=1
    )

    last = PLANE - 1
    oldest = lax.dynamic_index_in_dim(collected[hops], slot ^ last, 0, keepdims=True)
    far_blocks = collected[:hops] + [oldest]
    far_count = hops * PLANE * rows
    oldest_pos = (PLANE * (plane - hops) + last) * rows + jnp.arange(rows, dtype=jnp.int32)
    far_key_pos = jnp.concatenate([key_pos[:, :far_count], oldest_pos[None]], axis=1)
    far_key_doc = jnp.concatenate(
        [key_doc[:, :far_count], oldest[0, rows, :rows].astype(jnp.int32)[None]], axis=1
    )

    offsets_in_shard = jnp.arange(rows, dtype=jnp.int32).reshape(rows, 1)
    visit_pos = (my_index + PLANE * far) * rows + offsets_in_shard
    visit_doc = visiting[rows, :rows].astype(jnp.int32).reshape(rows, 1)
    visit_out, visit_stats, visit_rows = partial(
        visiting, far_blocks, far_key_pos, far_key_doc, visit_pos, visit_doc, jnp.bfloat16
    )
    ahead = [(s, s + PLANE * far) for s in range(ctx - PLANE * far)]
    far_out = lax.ppermute(visit_out, "ctx", ahead)
    far_rows = lax.ppermute(visit_rows, "ctx", ahead)

    query_pos = my_index * rows + offsets_in_shard
    near_out, near_stats, _ = partial(
        queries, blocks, key_pos, key_doc, query_pos, docs.reshape(rows, 1), jnp.bfloat16
    )
    has_far = plane >= far
    heads = near_stats.shape[1] // 2
    kind = jnp.arange(2 * heads, dtype=jnp.int32)[:, None]
    far_rows = jnp.where(has_far, far_rows, jnp.where(kind < heads, neg_large, 0.0))
    chunks = merge(near_out, near_stats, far_out, far_rows, out_weight, tp)

    received = lax.all_to_all(chunks, "tp", 0, 0, tiled=True)
    mixed = jnp.sum(received.astype(jnp.float32), axis=0)
    return mixed.astype(jnp.bfloat16)


def solution(mesh):
    placed = (P("ctx", "tp"), P("ctx", "tp"), P("ctx", "tp"), P("ctx"), P("tp", None))
    return jax.shard_map(
        shards, mesh=mesh, in_specs=placed, out_specs=P("ctx", "tp"), check_vma=False
    )
```
